32 devices in a mesh: src: 2 (over core), rows: 16 (over z, y, x).
Axes of the slice: x: 2, y: 2, z: 4, core: 2. Of those that a mesh axis runs over, the one named last changes fastest.
Arguments:
- slip_units: int32 [512, 2000], P(None, 'src'), may hold values from 0 to 15
- slip_scales: float32 [512, 16], P(None, 'src'), may hold values from 0.02 to 0.2
- green: bfloat16 [2000, 491520], P('src', 'rows'), may hold values from -0.08944272 to 0.08944272
- coast_gauges: int32 [2048, 8], replicated, may hold values from 0 to 2047
- coast_amps: float32 [2048, 8], replicated, may hold values from 0.05 to 0.3
- coast_counts: int32 [2048], replicated, may hold values from 1 to 8
Outputs:
- onshore: float32 [512, 2048], P('src', 'rows')
The draws below stay inside these ranges and needn't reach their ends.
Inputs may be any that keep to these rules, and one draw needn't show every extreme that they name: coast_gauges names gauges.
All inputs are finite; a program needn't handle non-finite values.
Results may differ from the reference program's by a relative error of at most 0.0039.
Values may be sent and summed in bfloat16 or wider, within the bound.
No kernel may reach another device: no remote copies, remote signals or barrier semaphores. Data moves between devices by JAX's collectives and lax.ppermute only.
A program may use at most 192 MiB of HBM per device.

```python
import math
import jax
import jax.numpy as jnp
from jax import lax

U = 2000
NG = 2048
NT = 240
UBLK = 125
K = 8
S = 512
NBLK = 16
TILES = 2048
N_SRC = 2
N_ROWS = 16


def draw_green(key, part):
    base_key = jax.random.fold_in(jax.random.fold_in(key, 7), 0)
    limit = 4.0 / math.sqrt(U)
    values = jax.random.normal(base_key, (U, NG * NT), jnp.float32) * (1.0 / math.sqrt(U))
    values = jnp.clip(values, -limit, limit)
    return values.astype(jnp.bfloat16)


def with_ends(result, stream_key, least, top_value):
    index_at = [jax.random.randint(jax.random.fold_in(stream_key, axis), (), 0, length) for axis, length in enumerate(result.shape)]
    main_axis = result.shape.index(max(result.shape))
    beside = index_at[:main_axis] + [(index_at[main_axis] + 1) % result.shape[main_axis]] + index_at[main_axis + 1:]
    return result.at[tuple(index_at)].set(least).at[tuple(beside)].set(top_value)


def steps_of(stream_key, extent, pieces, least, high):
    def one(dim, shards_of):
        heights = jax.random.uniform(jax.random.fold_in(jax.random.fold_in(stream_key, 6), dim), (shards_of,), jnp.float32, least / len(pieces), high / len(pieces))
        return jnp.repeat(jnp.exp(heights), extent[dim] // shards_of).reshape((-1,) + (1,) * (len(extent) - dim - 1))

    level = one(*pieces[0])
    for cut in pieces[1:]:
        level = level * one(*cut)
    return level


def setup_inputs(seed: int = 0) -> dict:
    seeds = jax.random.split(jax.random.key(seed), 7)
    slip_units = with_ends(jax.random.randint(seeds[0], (S, U), 0, 16), jax.random.fold_in(seeds[0], 1), 0, 15).astype(jnp.int32)
    slip_scales = jnp.clip(jnp.exp(math.log(0.2) - 2.3025851 * jax.random.uniform(seeds[1], (S, NBLK), jnp.float32) ** steps_of(seeds[1], (S, NBLK), ((1, 2),), -0.2, 0.2)), 0.02, 0.2)
    green = draw_green(jax.random.fold_in(seeds[6], 71), 0)
    coast_gauges = with_ends(jax.random.randint(seeds[3], (TILES, K), 0, NG), jax.random.fold_in(seeds[3], 1), 0, NG - 1).astype(jnp.int32)
    coast_amps = jnp.clip(jax.random.uniform(seeds[4], (TILES, K), jnp.float32, 0.05, 0.3), 0.05, 0.3)
    coast_counts = with_ends(jax.random.randint(seeds[5], (TILES,), 1, K + 1), jax.random.fold_in(seeds[5], 1), 1, K).astype(jnp.int32)
    return {"slip_units": slip_units, "slip_scales": slip_scales, "green": green, "coast_gauges": coast_gauges, "coast_amps": coast_amps, "coast_counts": coast_counts}


def reference(slip_units, slip_scales, green, coast_gauges, coast_amps, coast_counts):
    slip_weights = (slip_units.astype(jnp.float32).reshape(S, NBLK, UBLK) * slip_scales[:, :, None]).reshape(S, U).astype(jnp.bfloat16)
    group_size = U // N_SRC
    gauge_share = NG // N_ROWS
    column_share = gauge_share * NT

    def gauge_block(slab_index):
        column_block = lax.dynamic_slice_in_dim(green, slab_index * column_share, column_share, 1)
        summed = jnp.zeros((S, column_share), jnp.float32)
        for group in range(N_SRC):
            partial_value = jnp.dot(slip_weights[:, group * group_size:(group + 1) * group_size], column_block[group * group_size:(group + 1) * group_size], preferred_element_type=jnp.float32)
            rounded = lax.optimization_barrier(partial_value.astype(jnp.bfloat16))
            summed = summed + rounded.astype(jnp.float32)
        return jnp.max(jnp.abs(summed.reshape(S, gauge_share, NT)), axis=2)

    blocks = lax.map(gauge_block, jnp.arange(N_ROWS, dtype=jnp.int32))
    peak_values = jnp.transpose(blocks, (1, 0, 2)).reshape(S, NG)
    active_slot = jnp.arange(K, dtype=jnp.int32)[None, :] < coast_counts[:, None]
    weights = jnp.where(active_slot, coast_amps, jnp.zeros_like(coast_amps))
    picked = peak_values[:, coast_gauges]
    return jnp.sum(picked * weights[None, :, :], axis=2)
```

```python
import jax
import jax.numpy as jnp
from jax import lax
from jax.experimental import pallas as pl
from jax.sharding import PartitionSpec as P

NT = 240
UBLK = 125
SEG = 1920


def peak_kernel(mine_ref, recv_ref, out_ref):
    wave = mine_ref[...].astype(jnp.float32) + recv_ref[...].astype(jnp.float32)
    flipped = jnp.abs(wave).T
    gauges = SEG // NT
    out_ref[...] = jnp.max(flipped.reshape(gauges, NT, flipped.shape[1]), axis=1)


def peaks_of(mine, recv):
    rows, cols = mine.shape
    blocks = cols // SEG
    gauges = SEG // NT
    band = 128 if rows % 128 == 0 else rows
    return pl.pallas_call(
        peak_kernel,
        grid=(blocks, rows // band),
        in_specs=[pl.BlockSpec((band, SEG), lambda j, i: (i, j))] * 2,
        out_specs=pl.BlockSpec((gauges, band), lambda j, i: (j, i)),
        out_shape=jax.ShapeDtypeStruct((blocks * gauges, rows), jnp.float32),
        cost_estimate=pl.CostEstimate(
            flops=3 * rows * cols, transcendentals=0, bytes_accessed=4 * rows * cols
        ),
    )(mine, recv)


def body(slip_units, slip_scales, green, coast_gauges, coast_amps, coast_counts):
    scenarios = slip_units.shape[0]
    sources_here = slip_units.shape[1]
    block_count = slip_scales.shape[1]
    slip_weights = (
        (
            slip_units.astype(jnp.float32).reshape(scenarios, block_count, UBLK)
            * slip_scales[:, :, None]
        )
        .reshape(scenarios, sources_here)
        .astype(jnp.bfloat16)
    )
    me = lax.axis_index("src")
    groups = lax.axis_size("src")
    portion = scenarios // groups
    slip_mine = lax.dynamic_slice_in_dim(slip_weights, me * portion, portion, 0)
    slip_other = lax.dynamic_slice_in_dim(slip_weights, (1 - me) * portion, portion, 0)
    pairs = [(0, 1), (1, 0)]

    columns = green.shape[1]
    segments = columns // SEG
    chunks = max(c for c in (1, 2, 4) if segments % c == 0)
    width = columns // chunks
    pieces = []
    for c in range(chunks):
        block = green[:, c * width:(c + 1) * width]
        other = jnp.dot(slip_other, block, preferred_element_type=jnp.float32).astype(jnp.bfloat16)
        received = lax.ppermute(other, "src", pairs)
        mine = jnp.dot(slip_mine, block, preferred_element_type=jnp.float32).astype(jnp.bfloat16)
        pieces.append(peaks_of(mine, received))
    peaks_t = jnp.concatenate(pieces, axis=0) if chunks > 1 else pieces[0]

    tile_total = coast_gauges.shape[0]
    slot_count = coast_gauges.shape[1]
    owners = lax.axis_size("rows")
    tiles_here = tile_total // owners
    gauge_total = peaks_t.shape[0] * owners
    active_slot = jnp.arange(slot_count, dtype=jnp.int32)[None, :] < coast_counts[:, None]
    weights = jnp.where(active_slot, coast_amps, jnp.zeros_like(coast_amps))
    gathered = lax.all_gather(peaks_t, "rows", axis=0, tiled=True)
    first_tile = lax.axis_index("rows") * tiles_here
    mine_gauges = lax.dynamic_slice_in_dim(coast_gauges, first_tile, tiles_here, 0)
    mine_weights = lax.dynamic_slice_in_dim(weights, first_tile, tiles_here, 0)
    matches = mine_gauges[:, :, None] == jnp.arange(gauge_total, dtype=jnp.int32)[None, None, :]
    tile_table = jnp.sum(jnp.where(matches, mine_weights[:, :, None], 0.0), axis=1)
    onshore = lax.dot_general(
        gathered,
        tile_table,
        (((0,), (1,)), ((), ())),
        precision=lax.Precision.HIGHEST,
        preferred_element_type=jnp.float32,
    )
    return onshore


def solution(mesh):
    in_specs = (P(None, "src"), P(None, "src"), P("src", "rows"), P(), P(), P())
    out_specs = P("src", "rows")
    return jax.shard_map(body, mesh=mesh, in_specs=in_specs, out_specs=out_specs, check_vma=False)
```

```python
import numpy as np
import jax
import jax.numpy as jnp
from jax import lax
from jax.experimental import pallas as pl
from jax.experimental.pallas import tpu as pltpu
from jax.sharding import PartitionSpec as P

NT = 240
UBLK = 125
SEG = 1920


def matmul_kernel(slip_ref, green_ref, other_ref, mine_ref):
    half = other_ref.shape[0]
    product = jnp.dot(slip_ref[...], green_ref[...], preferred_element_type=jnp.float32)
    other_ref[...] = product[:half].astype(jnp.bfloat16)
    mine_ref[...] = product[half:].astype(jnp.bfloat16)


def partials_of(slip_ordered, green, chunk, width, tile):
    scenarios, sources = slip_ordered.shape
    half = scenarios // 2
    steps = width // tile
    return pl.pallas_call(
        matmul_kernel,
        grid=(steps,),
        in_specs=[
            pl.BlockSpec((scenarios, sources), lambda j: (0, 0)),
            pl.BlockSpec((sources, tile), lambda j: (0, chunk * steps + j)),
        ],
        out_specs=[pl.BlockSpec((half, tile), lambda j: (0, j))] * 2,
        out_shape=[jax.ShapeDtypeStruct((half, width), jnp.bfloat16)] * 2,
        cost_estimate=pl.CostEstimate(
            flops=2 * scenarios * sources * width,
            transcendentals=0,
            bytes_accessed=2 * (sources * width + scenarios * width),
        ),
    )(slip_ordered, green)


def peak_kernel(mine_ref, recv_ref, out_ref):
    wave = mine_ref[...].astype(jnp.float32) + recv_ref[...].astype(jnp.float32)
    flipped = jnp.abs(wave).T
    gauges = SEG // NT
    out_ref[...] = jnp.max(flipped.reshape(gauges, NT, flipped.shape[1]), axis=1)


def peaks_of(mine, recv):
    rows, cols = mine.shape
    blocks = cols // SEG
    gauges = SEG // NT
    band = 128 if rows % 128 == 0 else rows
    return pl.pallas_call(
        peak_kernel,
        grid=(blocks, rows // band),
        in_specs=[pl.BlockSpec((band, SEG), lambda j, i: (i, j))] * 2,
        out_specs=pl.BlockSpec((gauges, band), lambda j, i: (j, i)),
        out_shape=jax.ShapeDtypeStruct((blocks * gauges, rows), jnp.float32),
        cost_estimate=pl.CostEstimate(
            flops=3 * rows * cols, transcendentals=0, bytes_accessed=4 * rows * cols
        ),
    )(mine, recv)


def doubling_masks(owners):
    masks = []
    m = 1
    while m < owners:
        masks.append(m)
        m *= 2
    return masks[::-1]


def gather_rows(block, owners):
    me = lax.axis_index("rows")
    held = block
    for m in doubling_masks(owners):
        pairs = [(i, i ^ m) for i in range(owners)]
        got = lax.ppermute(held, "rows", pairs)
        upper = (me & m) != 0
        held = jnp.where(
            upper, jnp.concatenate([got, held], 0), jnp.concatenate([held, got], 0)
        )
    return held


def arrival_order(owners):
    order = [0]
    for m in doubling_masks(owners):
        order = order + [d ^ m for d in order]
    return order


def body(slip_units, slip_scales, green, coast_gauges, coast_amps, coast_counts):
    scenarios = slip_units.shape[0]
    sources_here = slip_units.shape[1]
    block_count = slip_scales.shape[1]
    slip_weights = (
        (
            slip_units.astype(jnp.float32).reshape(scenarios, block_count, UBLK)
            * slip_scales[:, :, None]
        )
        .reshape(scenarios, sources_here)
        .astype(jnp.bfloat16)
    )
    me = lax.axis_index("src")
    groups = lax.axis_size("src")
    portion = scenarios // groups
    slip_mine = lax.dynamic_slice_in_dim(slip_weights, me * portion, portion, 0)
    slip_other = lax.dynamic_slice_in_dim(slip_weights, (1 - me) * portion, portion, 0)
    slip_ordered = jnp.concatenate([slip_other, slip_mine], 0)
    pairs = [(0, 1), (1, 0)]

    owners = lax.axis_size("rows")
    columns = green.shape[1]
    gauges_here = columns // NT
    segments = columns // SEG
    chunks = max(c for c in (1, 2, 4) if segments % c == 0)
    width = columns // chunks
    tile = SEG
    per_chunk = gauges_here // chunks
    order = arrival_order(owners)
    pieces = []
    ids = []
    for c in range(chunks):
        other, mine = partials_of(slip_ordered, green, c, width, tile)
        received = lax.ppermute(other, "src", pairs)
        peaks_c = peaks_of(mine, received)
        pieces.append(gather_rows(peaks_c, owners))
        ids.append(
            (np.asarray(order)[:, None] * gauges_here + c * per_chunk + np.arange(per_chunk)[None, :]).reshape(-1)
        )
    gathered = jnp.concatenate(pieces, axis=0) if chunks > 1 else pieces[0]
    gauge_ids = jnp.asarray(np.concatenate(ids).astype(np.int32))

    tile_total = coast_gauges.shape[0]
    slot_count = coast_gauges.shape[1]
    tiles_here = tile_total // owners
    active_slot = jnp.arange(slot_count, dtype=jnp.int32)[None, :] < coast_counts[:, None]
    weights = jnp.where(active_slot, coast_amps, jnp.zeros_like(coast_amps))
    first_tile = lax.axis_index("rows") * tiles_here
    mine_gauges = lax.dynamic_slice_in_dim(coast_gauges, first_tile, tiles_here, 0)
    mine_weights = lax.dynamic_slice_in_dim(weights, first_tile, tiles_here, 0)
    matches = mine_gauges[:, :, None] == gauge_ids[None, None, :]
    tile_table = jnp.sum(jnp.where(matches, mine_weights[:, :, None], 0.0), axis=1)
    onshore = lax.dot_general(
        gathered,
        tile_table,
        (((0,), (1,)), ((), ())),
        precision=lax.Precision.HIGHEST,
        preferred_element_type=jnp.float32,
    )
    return onshore


def solution(mesh):
    in_specs = (P(None, "src"), P(None, "src"), P("src", "rows"), P(), P(), P())
    out_specs = P("src", "rows")
    return jax.shard_map(body, mesh=mesh, in_specs=in_specs, out_specs=out_specs, check_vma=False)
```

```python
import numpy as np
import jax
import jax.numpy as jnp
from jax import lax
from jax.experimental import pallas as pl
from jax.experimental.pallas import tpu as pltpu
from jax.sharding import PartitionSpec as P

NT = 240
UBLK = 125
SEG = 1920


def matmul_kernel(slip_ref, green_ref, other_ref, mine_ref):
    half = other_ref.shape[1]
    product = lax.dot_general(
        green_ref[...], slip_ref[...], (((0,), (0,)), ((), ())), preferred_element_type=jnp.float32
    )
    other_ref[...] = product[:, :half].astype(jnp.bfloat16)
    mine_ref[...] = product[:, half:].astype(jnp.bfloat16)


def partials_of(slip_ordered, green, chunk, width, tile):
    sources, scenarios = slip_ordered.shape
    half = scenarios // 2
    steps = width // tile
    return pl.pallas_call(
        matmul_kernel,
        grid=(steps,),
        in_specs=[
            pl.BlockSpec((sources, scenarios), lambda j: (0, 0)),
            pl.BlockSpec((sources, tile), lambda j: (0, chunk * steps + j)),
        ],
        out_specs=[pl.BlockSpec((tile, half), lambda j: (j, 0))] * 2,
        out_shape=[jax.ShapeDtypeStruct((width, half), jnp.bfloat16)] * 2,
        cost_estimate=pl.CostEstimate(
            flops=2 * scenarios * sources * width,
            transcendentals=0,
            bytes_accessed=2 * (sources * width + scenarios * width),
        ),
    )(slip_ordered, green)


def peak_kernel(mine_ref, recv_ref, out_ref):
    wave = mine_ref[...].astype(jnp.float32) + recv_ref[...].astype(jnp.float32)
    gauges = SEG // NT
    out_ref[...] = jnp.max(jnp.abs(wave).reshape(gauges, NT, wave.shape[1]), axis=1)


def peaks_of(mine, recv):
    cols, rows = mine.shape
    blocks = cols // SEG
    gauges = SEG // NT
    return pl.pallas_call(
        peak_kernel,
        grid=(blocks,),
        in_specs=[pl.BlockSpec((SEG, rows), lambda j: (j, 0))] * 2,
        out_specs=pl.BlockSpec((gauges, rows), lambda j: (j, 0)),
        out_shape=jax.ShapeDtypeStruct((blocks * gauges, rows), jnp.float32),
        cost_estimate=pl.CostEstimate(
            flops=3 * rows * cols, transcendentals=0, bytes_accessed=4 * rows * cols
        ),
    )(mine, recv)


def doubling_masks(owners):
    masks = []
    m = 1
    while m < owners:
        masks.append(m)
        m *= 2
    return masks[::-1]


def gather_rows(block, owners):
    me = lax.axis_index("rows")
    held = block
    for m in doubling_masks(owners):
        pairs = [(i, i ^ m) for i in range(owners)]
        got = lax.ppermute(held, "rows", pairs)
        upper = (me & m) != 0
        held = jnp.where(
            upper, jnp.concatenate([got, held], 0), jnp.concatenate([held, got], 0)
        )
    return held


def arrival_order(owners):
    order = [0]
    for m in doubling_masks(owners):
        order = order + [d ^ m for d in order]
    return order


def body(slip_units, slip_scales, green, coast_gauges, coast_amps, coast_counts):
    scenarios = slip_units.shape[0]
    units_t = slip_units.T.astype(jnp.float32)
    scale_rows = jnp.repeat(slip_scales.T, UBLK, axis=0)
    slip_t = (units_t * scale_rows).astype(jnp.bfloat16)
    me = lax.axis_index("src")
    groups = lax.axis_size("src")
    portion = scenarios // groups
    slip_mine = lax.dynamic_slice_in_dim(slip_t, me * portion, portion, 1)
    slip_other = lax.dynamic_slice_in_dim(slip_t, (1 - me) * portion, portion, 1)
    slip_ordered = jnp.concatenate([slip_other, slip_mine], 1)
    pairs = [(0, 1), (1, 0)]

    owners = lax.axis_size("rows")
    columns = green.shape[1]
    gauges_here = columns // NT
    segments = columns // SEG
    chunks = max(c for c in (1, 2, 4) if segments % c == 0)
    width = columns // chunks
    tile = SEG
    per_chunk = gauges_here // chunks
    order = arrival_order(owners)
    pieces = []
    ids = []
    for c in range(chunks):
        other, mine = partials_of(slip_ordered, green, c, width, tile)
        received = lax.ppermute(other, "src", pairs)
        peaks_c = peaks_of(mine, received)
        pieces.append(gather_rows(peaks_c, owners))
        ids.append(
            (np.asarray(order)[:, None] * gauges_here + c * per_chunk + np.arange(per_chunk)[None, :]).reshape(-1)
        )
    gathered = jnp.concatenate(pieces, axis=0) if chunks > 1 else pieces[0]
    gauge_ids = jnp.asarray(np.concatenate(ids).astype(np.int32))

    tile_total = coast_gauges.shape[0]
    slot_count = coast_gauges.shape[1]
    tiles_here = tile_total // owners
    active_slot = jnp.arange(slot_count, dtype=jnp.int32)[None, :] < coast_counts[:, None]
    weights = jnp.where(active_slot, coast_amps, jnp.zeros_like(coast_amps))
    first_tile = lax.axis_index("rows") * tiles_here
    mine_gauges = lax.dynamic_slice_in_dim(coast_gauges, first_tile, tiles_here, 0)
    mine_weights = lax.dynamic_slice_in_dim(weights, first_tile, tiles_here, 0)
    matches = mine_gauges[:, :, None] == gauge_ids[None, None, :]
    tile_table = jnp.sum(jnp.where(matches, mine_weights[:, :, None], 0.0), axis=1)
    onshore = lax.dot_general(
        gathered,
        tile_table,
        (((0,), (1,)), ((), ())),
        precision=lax.Precision.HIGHEST,
        preferred_element_type=jnp.float32,
    )
    return onshore


def solution(mesh):
    in_specs = (P(None, "src"), P(None, "src"), P("src", "rows"), P(), P(), P())
    out_specs = P("src", "rows")
    return jax.shard_map(body, mesh=mesh, in_specs=in_specs, out_specs=out_specs, check_vma=False)
```

```python
import numpy as np
import jax
import jax.numpy as jnp
from jax import lax
from jax.experimental import pallas as pl
from jax.experimental.pallas import tpu as pltpu
from jax.sharding import PartitionSpec as P

NT = 240
UBLK = 125
SEG = 1920


def matmul_kernel(slip_ref, green_ref, other_ref, mine_ref):
    half = other_ref.shape[1]
    product = lax.dot_general(
        green_ref[...], slip_ref[...], (((0,), (0,)), ((), ())), preferred_element_type=jnp.float32
    )
    other_ref[...] = product[:, :half].astype(jnp.bfloat16)
    mine_ref[...] = product[:, half:].astype(jnp.bfloat16)


def partials_of(slip_ordered, green, chunk, width, tile):
    sources, scenarios = slip_ordered.shape
    half = scenarios // 2
    steps = width // tile
    return pl.pallas_call(
        matmul_kernel,
        grid=(steps,),
        in_specs=[
            pl.BlockSpec((sources, scenarios), lambda j: (0, 0)),
            pl.BlockSpec((sources, tile), lambda j: (0, chunk * steps + j)),
        ],
        out_specs=[pl.BlockSpec((tile, half), lambda j: (j, 0))] * 2,
        out_shape=[jax.ShapeDtypeStruct((width, half), jnp.bfloat16)] * 2,
        cost_estimate=pl.CostEstimate(
            flops=2 * scenarios * sources * width,
            transcendentals=0,
            bytes_accessed=2 * (sources * width + scenarios * width),
        ),
    )(slip_ordered, green)


def peak_kernel(mine_ref, recv_ref, out_ref):
    wave = mine_ref[...].astype(jnp.float32) + recv_ref[...].astype(jnp.float32)
    gauges = SEG // NT
    out_ref[...] = jnp.max(jnp.abs(wave).reshape(gauges, NT, wave.shape[1]), axis=1)


def fused_kernel(slip_ref, green_ref, mine_prev_ref, recv_prev_ref, other_ref, mine_ref, peaks_ref):
    matmul_kernel(slip_ref, green_ref, other_ref, mine_ref)
    peak_kernel(mine_prev_ref, recv_prev_ref, peaks_ref)


def fused_of(slip_ordered, green, chunk, width, mine_prev, recv_prev):
    sources, scenarios = slip_ordered.shape
    half = scenarios // 2
    steps = width // SEG
    gauges = SEG // NT
    return pl.pallas_call(
        fused_kernel,
        grid=(steps,),
        in_specs=[
            pl.BlockSpec((sources, scenarios), lambda j: (0, 0)),
            pl.BlockSpec((sources, SEG), lambda j: (0, chunk * steps + j)),
            pl.BlockSpec((SEG, half), lambda j: (j, 0)),
            pl.BlockSpec((SEG, half), lambda j: (j, 0)),
        ],
        out_specs=[
            pl.BlockSpec((SEG, half), lambda j: (j, 0)),
            pl.BlockSpec((SEG, half), lambda j: (j, 0)),
            pl.BlockSpec((gauges, half), lambda j: (j, 0)),
        ],
        out_shape=[
            jax.ShapeDtypeStruct((width, half), jnp.bfloat16),
            jax.ShapeDtypeStruct((width, half), jnp.bfloat16),
            jax.ShapeDtypeStruct((steps * gauges, half), jnp.float32),
        ],
        cost_estimate=pl.CostEstimate(
            flops=2 * scenarios * sources * width,
            transcendentals=0,
            bytes_accessed=2 * (sources * width + 2 * scenarios * width),
        ),
    )(slip_ordered, green, mine_prev, recv_prev)


def peaks_of(mine, recv):
    cols, rows = mine.shape
    blocks = cols // SEG
    gauges = SEG // NT
    return pl.pallas_call(
        peak_kernel,
        grid=(blocks,),
        in_specs=[pl.BlockSpec((SEG, rows), lambda j: (j, 0))] * 2,
        out_specs=pl.BlockSpec((gauges, rows), lambda j: (j, 0)),
        out_shape=jax.ShapeDtypeStruct((blocks * gauges, rows), jnp.float32),
        cost_estimate=pl.CostEstimate(
            flops=3 * rows * cols, transcendentals=0, bytes_accessed=4 * rows * cols
        ),
    )(mine, recv)


def doubling_masks(owners):
    masks = []
    m = 1
    while m < owners:
        masks.append(m)
        m *= 2
    return masks[::-1]


def gather_rows(block, owners):
    me = lax.axis_index("rows")
    held = block
    for m in doubling_masks(owners):
        pairs = [(i, i ^ m) for i in range(owners)]
        got = lax.ppermute(held, "rows", pairs)
        upper = (me & m) != 0
        held = jnp.where(
            upper, jnp.concatenate([got, held], 0), jnp.concatenate([held, got], 0)
        )
    return held


def arrival_order(owners):
    order = [0]
    for m in doubling_masks(owners):
        order = order + [d ^ m for d in order]
    return order


def body(slip_units, slip_scales, green, coast_gauges, coast_amps, coast_counts):
    scenarios = slip_units.shape[0]
    units_t = slip_units.T.astype(jnp.float32)
    scale_rows = jnp.repeat(slip_scales.T, UBLK, axis=0)
    slip_t = (units_t * scale_rows).astype(jnp.bfloat16)
    me = lax.axis_index("src")
    groups = lax.axis_size("src")
    portion = scenarios // groups
    slip_mine = lax.dynamic_slice_in_dim(slip_t, me * portion, portion, 1)
    slip_other = lax.dynamic_slice_in_dim(slip_t, (1 - me) * portion, portion, 1)
    slip_ordered = jnp.concatenate([slip_other, slip_mine], 1)
    pairs = [(0, 1), (1, 0)]

    owners = lax.axis_size("rows")
    columns = green.shape[1]
    gauges_here = columns // NT
    segments = columns // SEG
    chunks = max(c for c in (1, 2, 4) if segments % c == 0)
    width = columns // chunks
    tile = SEG
    per_chunk = gauges_here // chunks
    order = arrival_order(owners)
    lag = 2 if chunks > 2 else 0
    mines, receiveds, peaks = [], [], [None] * chunks
    for c in range(chunks):
        if lag and c >= lag:
            other, mine, peaks[c - lag] = fused_of(
                slip_ordered, green, c, width, mines[c - lag], receiveds[c - lag]
            )
        else:
            other, mine = partials_of(slip_ordered, green, c, width, tile)
        mines.append(mine)
        receiveds.append(lax.ppermute(other, "src", pairs))
    for c in range(chunks):
        if peaks[c] is None:
            peaks[c] = peaks_of(mines[c], receiveds[c])
    pieces = [gather_rows(p, owners) for p in peaks]
    ids = [
        (np.asarray(order)[:, None] * gauges_here + c * per_chunk + np.arange(per_chunk)[None, :]).reshape(-1)
        for c in range(chunks)
    ]
    gauge_ids = jnp.asarray(np.concatenate(ids).astype(np.int32))

    tile_total = coast_gauges.shape[0]
    slot_count = coast_gauges.shape[1]
    tiles_here = tile_total // owners
    active_slot = jnp.arange(slot_count, dtype=jnp.int32)[None, :] < coast_counts[:, None]
    weights = jnp.where(active_slot, coast_amps, jnp.zeros_like(coast_amps))
    first_tile = lax.axis_index("rows") * tiles_here
    mine_gauges = lax.dynamic_slice_in_dim(coast_gauges, first_tile, tiles_here, 0)
    mine_weights = lax.dynamic_slice_in_dim(weights, first_tile, tiles_here, 0)
    matches = mine_gauges[:, :, None] == gauge_ids[None, None, :]
    tile_table = jnp.sum(jnp.where(matches, mine_weights[:, :, None], 0.0), axis=1)
    span = owners * per_chunk
    onshore = None
    for c in range(chunks):
        term = lax.dot_general(
            pieces[c],
            tile_table[:, c * span:(c + 1) * span],
            (((0,), (1,)), ((), ())),
            precision=lax.Precision.HIGHEST,
            preferred_element_type=jnp.float32,
        )
        onshore = term if onshore is None else onshore + term
    return onshore


def solution(mesh):
    in_specs = (P(None, "src"), P(None, "src"), P("src", "rows"), P(), P(), P())
    out_specs = P("src", "rows")
    return jax.shard_map(body, mesh=mesh, in_specs=in_specs, out_specs=out_specs, check_vma=False)
```

```python
import numpy as np
import jax
import jax.numpy as jnp
from jax import lax
from jax.experimental import pallas as pl
from jax.experimental.pallas import tpu as pltpu
from jax.sharding import PartitionSpec as P

NT = 240
UBLK = 125
SEG = 1920


def matmul_kernel(slip_ref, green_ref, other_ref, mine_ref):
    half = other_ref.shape[1]
    product = lax.dot_general(
        green_ref[...], slip_ref[...], (((0,), (0,)), ((), ())), preferred_element_type=jnp.float32
    )
    other_ref[...] = product[:, :half].astype(jnp.bfloat16)
    mine_ref[...] = product[:, half:].astype(jnp.bfloat16)


def partials_of(slip_ordered, green, chunk, width, tile):
    sources, scenarios = slip_ordered.shape
    half = scenarios // 2
    steps = width // tile
    return pl.pallas_call(
        matmul_kernel,
        grid=(steps,),
        in_specs=[
            pl.BlockSpec((sources, scenarios), lambda j: (0, 0)),
            pl.BlockSpec((sources, tile), lambda j: (0, chunk * steps + j)),
        ],
        out_specs=[pl.BlockSpec((tile, half), lambda j: (j, 0))] * 2,
        out_shape=[jax.ShapeDtypeStruct((width, half), jnp.bfloat16)] * 2,
        cost_estimate=pl.CostEstimate(
            flops=2 * scenarios * sources * width,
            transcendentals=0,
            bytes_accessed=2 * (sources * width + scenarios * width),
        ),
    )(slip_ordered, green)


def peak_kernel(mine_ref, recv_ref, out_ref):
    wave = mine_ref[...].astype(jnp.float32) + recv_ref[...].astype(jnp.float32)
    gauges = SEG // NT
    out_ref[...] = jnp.max(jnp.abs(wave).reshape(gauges, NT, wave.shape[1]), axis=1)


def fused_kernel(slip_ref, green_ref, mine_prev_ref, recv_prev_ref, other_ref, mine_ref, peaks_ref):
    matmul_kernel(slip_ref, green_ref, other_ref, mine_ref)
    peak_kernel(mine_prev_ref, recv_prev_ref, peaks_ref)


def fused_of(slip_ordered, green, chunk, width, mine_prev, recv_prev):
    sources, scenarios = slip_ordered.shape
    half = scenarios // 2
    steps = width // SEG
    gauges = SEG // NT
    return pl.pallas_call(
        fused_kernel,
        grid=(steps,),
        in_specs=[
            pl.BlockSpec((sources, scenarios), lambda j: (0, 0)),
            pl.BlockSpec((sources, SEG), lambda j: (0, chunk * steps + j)),
            pl.BlockSpec((SEG, half), lambda j: (j, 0)),
            pl.BlockSpec((SEG, half), lambda j: (j, 0)),
        ],
        out_specs=[
            pl.BlockSpec((SEG, half), lambda j: (j, 0)),
            pl.BlockSpec((SEG, half), lambda j: (j, 0)),
            pl.BlockSpec((gauges, half), lambda j: (j, 0)),
        ],
        out_shape=[
            jax.ShapeDtypeStruct((width, half), jnp.bfloat16),
            jax.ShapeDtypeStruct((width, half), jnp.bfloat16),
            jax.ShapeDtypeStruct((steps * gauges, half), jnp.float32),
        ],
        cost_estimate=pl.CostEstimate(
            flops=2 * scenarios * sources * width,
            transcendentals=0,
            bytes_accessed=2 * (sources * width + 2 * scenarios * width),
        ),
    )(slip_ordered, green, mine_prev, recv_prev)


def peaks_of(mine, recv):
    cols, rows = mine.shape
    blocks = cols // SEG
    gauges = SEG // NT
    return pl.pallas_call(
        peak_kernel,
        grid=(blocks,),
        in_specs=[pl.BlockSpec((SEG, rows), lambda j: (j, 0))] * 2,
        out_specs=pl.BlockSpec((gauges, rows), lambda j: (j, 0)),
        out_shape=jax.ShapeDtypeStruct((blocks * gauges, rows), jnp.float32),
        cost_estimate=pl.CostEstimate(
            flops=3 * rows * cols, transcendentals=0, bytes_accessed=4 * rows * cols
        ),
    )(mine, recv)


def doubling_masks(owners):
    masks = []
    m = 1
    while m < owners:
        masks.append(m)
        m *= 2
    return masks[::-1]


def gather_rows(block, owners):
    me = lax.axis_index("rows")
    held = block
    for m in doubling_masks(owners):
        pairs = [(i, i ^ m) for i in range(owners)]
        got = lax.ppermute(held, "rows", pairs)
        upper = (me & m) != 0
        held = jnp.where(
            upper, jnp.concatenate([got, held], 0), jnp.concatenate([held, got], 0)
        )
    return held


def arrival_order(owners):
    order = [0]
    for m in doubling_masks(owners):
        order = order + [d ^ m for d in order]
    return order


def body(slip_units, slip_scales, green, coast_gauges, coast_amps, coast_counts):
    scenarios = slip_units.shape[0]
    units_t = slip_units.T.astype(jnp.float32)
    scale_rows = jnp.repeat(slip_scales.T, UBLK, axis=0)
    slip_t = (units_t * scale_rows).astype(jnp.bfloat16)
    me = lax.axis_index("src")
    groups = lax.axis_size("src")
    portion = scenarios // groups
    slip_mine = lax.dynamic_slice_in_dim(slip_t, me * portion, portion, 1)
    slip_other = lax.dynamic_slice_in_dim(slip_t, (1 - me) * portion, portion, 1)
    slip_ordered = jnp.concatenate([slip_other, slip_mine], 1)
    pairs = [(0, 1), (1, 0)]

    owners = lax.axis_size("rows")
    columns = green.shape[1]
    gauges_here = columns // NT
    segments = columns // SEG
    chunks = max(c for c in (1, 2, 4) if segments % c == 0)
    width = columns // chunks
    tile = SEG
    per_chunk = gauges_here // chunks
    order = arrival_order(owners)
    lag = 2 if chunks > 2 else 0
    mines, receiveds, peaks = [], [], [None] * chunks
    for c in range(chunks):
        if lag and c >= lag:
            other, mine, peaks[c - lag] = fused_of(
                slip_ordered, green, c, width, mines[c - lag], receiveds[c - lag]
            )
        else:
            other, mine = partials_of(slip_ordered, green, c, width, tile)
        mines.append(mine)
        receiveds.append(lax.ppermute(other, "src", pairs))
    for c in range(chunks):
        if peaks[c] is None:
            peaks[c] = peaks_of(mines[c], receiveds[c])
    split = (chunks + 1) // 2
    bundles = [list(range(split)), list(range(split, chunks))] if chunks > 1 else [[0]]
    pieces, ids = [], []
    for bundle in bundles:
        joined = jnp.concatenate([peaks[c] for c in bundle], 0) if len(bundle) > 1 else peaks[bundle[0]]
        pieces.append(gather_rows(joined, owners))
        local = np.concatenate([c * per_chunk + np.arange(per_chunk) for c in bundle])
        ids.append((np.asarray(order)[:, None] * gauges_here + local[None, :]).reshape(-1))
    gauge_ids = jnp.asarray(np.concatenate(ids).astype(np.int32))

    tile_total = coast_gauges.shape[0]
    slot_count = coast_gauges.shape[1]
    tiles_here = tile_total // owners
    active_slot = jnp.arange(slot_count, dtype=jnp.int32)[None, :] < coast_counts[:, None]
    weights = jnp.where(active_slot, coast_amps, jnp.zeros_like(coast_amps))
    first_tile = lax.axis_index("rows") * tiles_here
    mine_gauges = lax.dynamic_slice_in_dim(coast_gauges, first_tile, tiles_here, 0)
    mine_weights = lax.dynamic_slice_in_dim(weights, first_tile, tiles_here, 0)
    matches = mine_gauges[:, :, None] == gauge_ids[None, None, :]
    tile_table = jnp.sum(jnp.where(matches, mine_weights[:, :, None], 0.0), axis=1)
    onshore = None
    start = 0
    for piece in pieces:
        span = piece.shape[0]
        term = lax.dot_general(
            piece,
            tile_table[:, start:start + span],
            (((0,), (1,)), ((), ())),
            precision=lax.Precision.HIGHEST,
            preferred_element_type=jnp.float32,
        )
        start += span
        onshore = term if onshore is None else onshore + term
    return onshore


def solution(mesh):
    in_specs = (P(None, "src"), P(None, "src"), P("src", "rows"), P(), P(), P())
    out_specs = P("src", "rows")
    return jax.shard_map(body, mesh=mesh, in_specs=in_specs, out_specs=out_specs, check_vma=False)
```

```python
import functools

import numpy as np
import jax
import jax.numpy as jnp
from jax import lax
from jax.experimental import pallas as pl
from jax.experimental.pallas import tpu as pltpu
from jax.sharding import PartitionSpec as P

NT = 240
UBLK = 125
SEG = 1920


def matmul_kernel(slip_ref, green_ref, other_ref, mine_ref):
    half = other_ref.shape[1]
    product = lax.dot_general(
        green_ref[...], slip_ref[...], (((0,), (0,)), ((), ())), preferred_element_type=jnp.float32
    )
    other_ref[...] = product[:, :half].astype(jnp.bfloat16)
    mine_ref[...] = product[:, half:].astype(jnp.bfloat16)


def partials_of(slip_ordered, green, first, steps):
    sources, scenarios = slip_ordered.shape
    half = scenarios // 2
    tile = SEG
    width = steps * tile
    return pl.pallas_call(
        matmul_kernel,
        grid=(steps,),
        in_specs=[
            pl.BlockSpec((sources, scenarios), lambda j: (0, 0)),
            pl.BlockSpec((sources, tile), lambda j: (0, first + j)),
        ],
        out_specs=[pl.BlockSpec((tile, half), lambda j: (j, 0))] * 2,
        out_shape=[jax.ShapeDtypeStruct((width, half), jnp.bfloat16)] * 2,
        cost_estimate=pl.CostEstimate(
            flops=2 * scenarios * sources * width,
            transcendentals=0,
            bytes_accessed=2 * (sources * width + scenarios * width),
        ),
    )(slip_ordered, green)


def peak_kernel(mine_ref, recv_ref, out_ref):
    wave = mine_ref[...].astype(jnp.float32) + recv_ref[...].astype(jnp.float32)
    gauges = SEG // NT
    out_ref[...] = jnp.max(jnp.abs(wave).reshape(gauges, NT, wave.shape[1]), axis=1)


def fused_kernel(slip_ref, green_ref, mine_prev_ref, recv_prev_ref, other_ref, mine_ref, peaks_ref, *, trail):
    matmul_kernel(slip_ref, green_ref, other_ref, mine_ref)

    @pl.when(pl.program_id(0) < trail)
    def _():
        peak_kernel(mine_prev_ref, recv_prev_ref, peaks_ref)


def fused_of(slip_ordered, green, first, steps, mine_prev, recv_prev):
    sources, scenarios = slip_ordered.shape
    half = scenarios // 2
    trail = mine_prev.shape[0] // SEG
    gauges = SEG // NT
    back = lambda j: (jnp.minimum(j, trail - 1), 0)
    return pl.pallas_call(
        functools.partial(fused_kernel, trail=trail),
        grid=(steps,),
        in_specs=[
            pl.BlockSpec((sources, scenarios), lambda j: (0, 0)),
            pl.BlockSpec((sources, SEG), lambda j: (0, first + j)),
            pl.BlockSpec((SEG, half), back),
            pl.BlockSpec((SEG, half), back),
        ],
        out_specs=[
            pl.BlockSpec((SEG, half), lambda j: (j, 0)),
            pl.BlockSpec((SEG, half), lambda j: (j, 0)),
            pl.BlockSpec((gauges, half), back),
        ],
        out_shape=[
            jax.ShapeDtypeStruct((steps * SEG, half), jnp.bfloat16),
            jax.ShapeDtypeStruct((steps * SEG, half), jnp.bfloat16),
            jax.ShapeDtypeStruct((trail * gauges, half), jnp.float32),
        ],
        cost_estimate=pl.CostEstimate(
            flops=2 * scenarios * sources * steps * SEG,
            transcendentals=0,
            bytes_accessed=2 * (sources * steps * SEG + scenarios * (steps + trail) * SEG),
        ),
    )(slip_ordered, green, mine_prev, recv_prev)


def peaks_of(mine, recv):
    cols, rows = mine.shape
    blocks = cols // SEG
    gauges = SEG // NT
    return pl.pallas_call(
        peak_kernel,
        grid=(blocks,),
        in_specs=[pl.BlockSpec((SEG, rows), lambda j: (j, 0))] * 2,
        out_specs=pl.BlockSpec((gauges, rows), lambda j: (j, 0)),
        out_shape=jax.ShapeDtypeStruct((blocks * gauges, rows), jnp.float32),
        cost_estimate=pl.CostEstimate(
            flops=3 * rows * cols, transcendentals=0, bytes_accessed=4 * rows * cols
        ),
    )(mine, recv)


def doubling_masks(owners):
    masks = []
    m = 1
    while m < owners:
        masks.append(m)
        m *= 2
    return masks[::-1]


def gather_rows(block, owners):
    me = lax.axis_index("rows")
    held = block
    for m in doubling_masks(owners):
        pairs = [(i, i ^ m) for i in range(owners)]
        got = lax.ppermute(held, "rows", pairs)
        upper = (me & m) != 0
        held = jnp.where(
            upper, jnp.concatenate([got, held], 0), jnp.concatenate([held, got], 0)
        )
    return held


def chunk_plan(segments):
    if segments >= 8:
        rest = segments - 2
        size, extra = divmod(rest, 4)
        return [size] * (4 - extra) + [size + 1] * extra + [1, 1]
    return [1] * segments


def arrival_order(owners):
    order = [0]
    for m in doubling_masks(owners):
        order = order + [d ^ m for d in order]
    return order


def body(slip_units, slip_scales, green, coast_gauges, coast_amps, coast_counts):
    scenarios = slip_units.shape[0]
    units_t = slip_units.T.astype(jnp.float32)
    scale_rows = jnp.repeat(slip_scales.T, UBLK, axis=0)
    slip_t = (units_t * scale_rows).astype(jnp.bfloat16)
    me = lax.axis_index("src")
    groups = lax.axis_size("src")
    portion = scenarios // groups
    slip_mine = lax.dynamic_slice_in_dim(slip_t, me * portion, portion, 1)
    slip_other = lax.dynamic_slice_in_dim(slip_t, (1 - me) * portion, portion, 1)
    slip_ordered = jnp.concatenate([slip_other, slip_mine], 1)
    pairs = [(0, 1), (1, 0)]

    owners = lax.axis_size("rows")
    columns = green.shape[1]
    gauges_here = columns // NT
    segments = columns // SEG
    sizes = chunk_plan(segments)
    chunks = len(sizes)
    firsts = [sum(sizes[:c]) for c in range(chunks)]
    gauges_per_seg = SEG // NT
    order = arrival_order(owners)
    mines, receiveds, peaks = [], [], [None] * chunks
    for c in range(chunks):
        if c >= 2 and sizes[c - 2] <= sizes[c]:
            other, mine, peaks[c - 2] = fused_of(
                slip_ordered, green, firsts[c], sizes[c], mines[c - 2], receiveds[c - 2]
            )
        else:
            other, mine = partials_of(slip_ordered, green, firsts[c], sizes[c])
        mines.append(mine)
        receiveds.append(lax.ppermute(other, "src", pairs))
    for c in range(chunks):
        if peaks[c] is None:
            peaks[c] = peaks_of(mines[c], receiveds[c])
    bundles = [list(range(chunks - 2)), [chunks - 2, chunks - 1]] if chunks > 2 else [list(range(chunks))]
    pieces, ids = [], []
    for bundle in bundles:
        joined = jnp.concatenate([peaks[c] for c in bundle], 0) if len(bundle) > 1 else peaks[bundle[0]]
        pieces.append(gather_rows(joined, owners))
        local = np.concatenate(
            [firsts[c] * gauges_per_seg + np.arange(sizes[c] * gauges_per_seg) for c in bundle]
        )
        ids.append((np.asarray(order)[:, None] * gauges_here + local[None, :]).reshape(-1))
    gauge_ids = jnp.asarray(np.concatenate(ids).astype(np.int32))

    tile_total = coast_gauges.shape[0]
    slot_count = coast_gauges.shape[1]
    tiles_here = tile_total // owners
    active_slot = jnp.arange(slot_count, dtype=jnp.int32)[None, :] < coast_counts[:, None]
    weights = jnp.where(active_slot, coast_amps, jnp.zeros_like(coast_amps))
    first_tile = lax.axis_index("rows") * tiles_here
    mine_gauges = lax.dynamic_slice_in_dim(coast_gauges, first_tile, tiles_here, 0)
    mine_weights = lax.dynamic_slice_in_dim(weights, first_tile, tiles_here, 0)
    matches = mine_gauges[:, :, None] == gauge_ids[None, None, :]
    tile_table = jnp.sum(jnp.where(matches, mine_weights[:, :, None], 0.0), axis=1)
    onshore = None
    start = 0
    for piece in pieces:
        span = piece.shape[0]
        term = lax.dot_general(
            piece,
            tile_table[:, start:start + span],
            (((0,), (1,)), ((), ())),
            precision=lax.Precision.HIGHEST,
            preferred_element_type=jnp.float32,
        )
        start += span
        onshore = term if onshore is None else onshore + term
    return onshore


def solution(mesh):
    in_specs = (P(None, "src"), P(None, "src"), P("src", "rows"), P(), P(), P())
    out_specs = P("src", "rows")
    return jax.shard_map(body, mesh=mesh, in_specs=in_specs, out_specs=out_specs, check_vma=False)
```

```python
import numpy as np
import jax
import jax.numpy as jnp
from jax import lax
from jax.experimental import pallas as pl
from jax.experimental.pallas import tpu as pltpu
from jax.sharding import PartitionSpec as P

NT = 240
UBLK = 125
SEG = 1920


def matmul_kernel(slip_ref, green_ref, other_ref, mine_ref):
    half = other_ref.shape[1]
    product = lax.dot_general(
        green_ref[...], slip_ref[...], (((0,), (0,)), ((), ())), preferred_element_type=jnp.float32
    )
    other_ref[...] = product[:, :half].astype(jnp.bfloat16)
    mine_ref[...] = product[:, half:].astype(jnp.bfloat16)


def partials_of(slip_ordered, green, chunk, width, tile):
    sources, scenarios = slip_ordered.shape
    half = scenarios // 2
    steps = width // tile
    return pl.pallas_call(
        matmul_kernel,
        grid=(steps,),
        in_specs=[
            pl.BlockSpec((sources, scenarios), lambda j: (0, 0)),
            pl.BlockSpec((sources, tile), lambda j: (0, chunk * steps + j)),
        ],
        out_specs=[pl.BlockSpec((tile, half), lambda j: (j, 0))] * 2,
        out_shape=[jax.ShapeDtypeStruct((width, half), jnp.bfloat16)] * 2,
        cost_estimate=pl.CostEstimate(
            flops=2 * scenarios * sources * width,
            transcendentals=0,
            bytes_accessed=2 * (sources * width + scenarios * width),
        ),
    )(slip_ordered, green)


def peak_kernel(mine_ref, recv_ref, out_ref):
    wave = mine_ref[...].astype(jnp.float32) + recv_ref[...].astype(jnp.float32)
    gauges = SEG // NT
    out_ref[...] = jnp.max(jnp.abs(wave).reshape(gauges, NT, wave.shape[1]), axis=1)


def fused_kernel(slip_ref, green_ref, mine_prev_ref, recv_prev_ref, other_ref, mine_ref, peaks_ref):
    matmul_kernel(slip_ref, green_ref, other_ref, mine_ref)
    peak_kernel(mine_prev_ref, recv_prev_ref, peaks_ref)


def fused_of(slip_ordered, green, chunk, width, mine_prev, recv_prev):
    sources, scenarios = slip_ordered.shape
    half = scenarios // 2
    steps = width // SEG
    gauges = SEG // NT
    return pl.pallas_call(
        fused_kernel,
        grid=(steps,),
        in_specs=[
            pl.BlockSpec((sources, scenarios), lambda j: (0, 0)),
            pl.BlockSpec((sources, SEG), lambda j: (0, chunk * steps + j)),
            pl.BlockSpec((SEG, half), lambda j: (j, 0)),
            pl.BlockSpec((SEG, half), lambda j: (j, 0)),
        ],
        out_specs=[
            pl.BlockSpec((SEG, half), lambda j: (j, 0)),
            pl.BlockSpec((SEG, half), lambda j: (j, 0)),
            pl.BlockSpec((gauges, half), lambda j: (j, 0)),
        ],
        out_shape=[
            jax.ShapeDtypeStruct((width, half), jnp.bfloat16),
            jax.ShapeDtypeStruct((width, half), jnp.bfloat16),
            jax.ShapeDtypeStruct((steps * gauges, half), jnp.float32),
        ],
        cost_estimate=pl.CostEstimate(
            flops=2 * scenarios * sources * width,
            transcendentals=0,
            bytes_accessed=2 * (sources * width + 2 * scenarios * width),
        ),
    )(slip_ordered, green, mine_prev, recv_prev)


def peaks_of(mine, recv):
    cols, rows = mine.shape
    blocks = cols // SEG
    gauges = SEG // NT
    return pl.pallas_call(
        peak_kernel,
        grid=(blocks,),
        in_specs=[pl.BlockSpec((SEG, rows), lambda j: (j, 0))] * 2,
        out_specs=pl.BlockSpec((gauges, rows), lambda j: (j, 0)),
        out_shape=jax.ShapeDtypeStruct((blocks * gauges, rows), jnp.float32),
        cost_estimate=pl.CostEstimate(
            flops=3 * rows * cols, transcendentals=0, bytes_accessed=4 * rows * cols
        ),
    )(mine, recv)


def doubling_masks(owners):
    masks = []
    m = 1
    while m < owners:
        masks.append(m)
        m *= 2
    return masks[::-1]


def gather_rows(block, owners):
    me = lax.axis_index("rows")
    held = block.astype(jnp.bfloat16)
    for m in doubling_masks(owners):
        pairs = [(i, i ^ m) for i in range(owners)]
        got = lax.ppermute(held, "rows", pairs)
        upper = (me & m) != 0
        held = jnp.where(
            upper, jnp.concatenate([got, held], 0), jnp.concatenate([held, got], 0)
        )
    return held.astype(jnp.float32)


def arrival_order(owners):
    order = [0]
    for m in doubling_masks(owners):
        order = order + [d ^ m for d in order]
    return order


def body(slip_units, slip_scales, green, coast_gauges, coast_amps, coast_counts):
    scenarios = slip_units.shape[0]
    units_t = slip_units.T.astype(jnp.float32)
    scale_rows = jnp.repeat(slip_scales.T, UBLK, axis=0)
    slip_t = (units_t * scale_rows).astype(jnp.bfloat16)
    me = lax.axis_index("src")
    groups = lax.axis_size("src")
    portion = scenarios // groups
    slip_mine = lax.dynamic_slice_in_dim(slip_t, me * portion, portion, 1)
    slip_other = lax.dynamic_slice_in_dim(slip_t, (1 - me) * portion, portion, 1)
    slip_ordered = jnp.concatenate([slip_other, slip_mine], 1)
    pairs = [(0, 1), (1, 0)]

    owners = lax.axis_size("rows")
    columns = green.shape[1]
    gauges_here = columns // NT
    segments = columns // SEG
    chunks = max(c for c in (1, 2, 4) if segments % c == 0)
    width = columns // chunks
    tile = SEG
    per_chunk = gauges_here // chunks
    order = arrival_order(owners)
    lag = 2 if chunks > 2 else 0
    mines, receiveds, peaks = [], [], [None] * chunks
    for c in range(chunks):
        if lag and c >= lag:
            other, mine, peaks[c - lag] = fused_of(
                slip_ordered, green, c, width, mines[c - lag], receiveds[c - lag]
            )
        else:
            other, mine = partials_of(slip_ordered, green, c, width, tile)
        mines.append(mine)
        receiveds.append(lax.ppermute(other, "src", pairs))
    for c in range(chunks):
        if peaks[c] is None:
            peaks[c] = peaks_of(mines[c], receiveds[c])
    split = (chunks + 1) // 2
    bundles = [list(range(split)), list(range(split, chunks))] if chunks > 1 else [[0]]
    pieces, ids = [], []
    for bundle in bundles:
        joined = jnp.concatenate([peaks[c] for c in bundle], 0) if len(bundle) > 1 else peaks[bundle[0]]
        pieces.append(gather_rows(joined, owners))
        local = np.concatenate([c * per_chunk + np.arange(per_chunk) for c in bundle])
        ids.append((np.asarray(order)[:, None] * gauges_here + local[None, :]).reshape(-1))
    gauge_ids = jnp.asarray(np.concatenate(ids).astype(np.int32))

    tile_total = coast_gauges.shape[0]
    slot_count = coast_gauges.shape[1]
    tiles_here = tile_total // owners
    active_slot = jnp.arange(slot_count, dtype=jnp.int32)[None, :] < coast_counts[:, None]
    weights = jnp.where(active_slot, coast_amps, jnp.zeros_like(coast_amps))
    first_tile = lax.axis_index("rows") * tiles_here
    mine_gauges = lax.dynamic_slice_in_dim(coast_gauges, first_tile, tiles_here, 0)
    mine_weights = lax.dynamic_slice_in_dim(weights, first_tile, tiles_here, 0)
    matches = mine_gauges[:, :, None] == gauge_ids[None, None, :]
    tile_table = jnp.sum(jnp.where(matches, mine_weights[:, :, None], 0.0), axis=1)
    onshore = None
    start = 0
    for piece in pieces:
        span = piece.shape[0]
        term = lax.dot_general(
            piece,
            tile_table[:, start:start + span],
            (((0,), (1,)), ((), ())),
            precision=lax.Precision.HIGHEST,
            preferred_element_type=jnp.float32,
        )
        start += span
        onshore = term if onshore is None else onshore + term
    return onshore


def solution(mesh):
    in_specs = (P(None, "src"), P(None, "src"), P("src", "rows"), P(), P(), P())
    out_specs = P("src", "rows")
    return jax.shard_map(body, mesh=mesh, in_specs=in_specs, out_specs=out_specs, check_vma=False)
```

```python
import numpy as np
import jax
import jax.numpy as jnp
from jax import lax
from jax.experimental import pallas as pl
from jax.experimental.pallas import tpu as pltpu
from jax.sharding import PartitionSpec as P

NT = 240
UBLK = 125
SEG = 1920


def half_kernel(slip_ref, green_ref, out_ref):
    product = lax.dot_general(
        green_ref[...], slip_ref[...], (((0,), (0,)), ((), ())), preferred_element_type=jnp.float32
    )
    out_ref[...] = product.astype(jnp.bfloat16)


def peak_kernel(mine_ref, recv_ref, out_ref):
    wave = mine_ref[...].astype(jnp.float32) + recv_ref[...].astype(jnp.float32)
    gauges = SEG // NT
    out_ref[...] = jnp.max(jnp.abs(wave).reshape(gauges, NT, wave.shape[1]), axis=1)


def fused_kernel(slip_ref, green_ref, mine_prev_ref, recv_prev_ref, out_ref, peaks_ref):
    half_kernel(slip_ref, green_ref, out_ref)
    peak_kernel(mine_prev_ref, recv_prev_ref, peaks_ref)


def half_of(slip_half, green, first, steps, previous=None):
    sources, half = slip_half.shape
    gauges = SEG // NT
    in_specs = [
        pl.BlockSpec((sources, half), lambda j: (0, 0)),
        pl.BlockSpec((sources, SEG), lambda j: (0, first + j)),
    ]
    out_specs = [pl.BlockSpec((SEG, half), lambda j: (j, 0))]
    out_shape = [jax.ShapeDtypeStruct((steps * SEG, half), jnp.bfloat16)]
    operands = [slip_half, green]
    kernel = half_kernel
    moved = 2 * (sources * steps * SEG + half * steps * SEG)
    if previous is not None:
        kernel = fused_kernel
        in_specs += [pl.BlockSpec((SEG, half), lambda j: (j, 0))] * 2
        out_specs.append(pl.BlockSpec((gauges, half), lambda j: (j, 0)))
        out_shape.append(jax.ShapeDtypeStruct((steps * gauges, half), jnp.float32))
        operands += list(previous)
        moved += 4 * half * steps * SEG
    result = pl.pallas_call(
        kernel,
        grid=(steps,),
        in_specs=in_specs,
        out_specs=out_specs,
        out_shape=out_shape,
        cost_estimate=pl.CostEstimate(
            flops=2 * half * sources * steps * SEG, transcendentals=0, bytes_accessed=moved
        ),
    )(*operands)
    return result if previous is not None else (result[0], None)


def peaks_of(mine, recv):
    cols, rows = mine.shape
    blocks = cols // SEG
    gauges = SEG // NT
    return pl.pallas_call(
        peak_kernel,
        grid=(blocks,),
        in_specs=[pl.BlockSpec((SEG, rows), lambda j: (j, 0))] * 2,
        out_specs=pl.BlockSpec((gauges, rows), lambda j: (j, 0)),
        out_shape=jax.ShapeDtypeStruct((blocks * gauges, rows), jnp.float32),
        cost_estimate=pl.CostEstimate(
            flops=3 * rows * cols, transcendentals=0, bytes_accessed=4 * rows * cols
        ),
    )(mine, recv)


def doubling_masks(owners):
    masks = []
    m = 1
    while m < owners:
        masks.append(m)
        m *= 2
    return masks[::-1]


def gather_rows(block, owners):
    me = lax.axis_index("rows")
    held = block.astype(jnp.bfloat16)
    for m in doubling_masks(owners):
        pairs = [(i, i ^ m) for i in range(owners)]
        got = lax.ppermute(held, "rows", pairs)
        upper = (me & m) != 0
        held = jnp.where(
            upper, jnp.concatenate([got, held], 0), jnp.concatenate([held, got], 0)
        )
    return held.astype(jnp.float32)


def arrival_order(owners):
    order = [0]
    for m in doubling_masks(owners):
        order = order + [d ^ m for d in order]
    return order


def body(slip_units, slip_scales, green, coast_gauges, coast_amps, coast_counts):
    scenarios = slip_units.shape[0]
    units_t = slip_units.T.astype(jnp.float32)
    scale_rows = jnp.repeat(slip_scales.T, UBLK, axis=0)
    slip_t = (units_t * scale_rows).astype(jnp.bfloat16)
    me = lax.axis_index("src")
    groups = lax.axis_size("src")
    portion = scenarios // groups
    slip_mine = lax.dynamic_slice_in_dim(slip_t, me * portion, portion, 1)
    slip_other = lax.dynamic_slice_in_dim(slip_t, (1 - me) * portion, portion, 1)
    pairs = [(0, 1), (1, 0)]

    owners = lax.axis_size("rows")
    columns = green.shape[1]
    gauges_here = columns // NT
    segments = columns // SEG
    chunks = max(c for c in (1, 2, 4) if segments % c == 0)
    width = columns // chunks
    tile = SEG
    per_chunk = gauges_here // chunks
    order = arrival_order(owners)
    steps = width // SEG
    mines, receiveds, peaks = [], [], [None] * chunks
    for c in range(chunks):
        prev_o = c - 2 if c >= 2 and c - 2 >= 0 and peaks[c - 2] is None else None
        if prev_o is not None:
            other, peaks[prev_o] = half_of(
                slip_other, green, c * steps, steps, (mines[prev_o], receiveds[prev_o])
            )
        else:
            other, _ = half_of(slip_other, green, c * steps, steps)
        receiveds.append(lax.ppermute(other, "src", pairs))
        prev_m = c - 1 if c >= 2 and peaks[c - 1] is None and c - 1 != prev_o else None
        if prev_m is not None:
            mine, peaks[prev_m] = half_of(
                slip_mine, green, c * steps, steps, (mines[prev_m], receiveds[prev_m])
            )
        else:
            mine, _ = half_of(slip_mine, green, c * steps, steps)
        mines.append(mine)
    for c in range(chunks):
        if peaks[c] is None:
            peaks[c] = peaks_of(mines[c], receiveds[c])
    split = (chunks + 1) // 2
    bundles = [list(range(split)), list(range(split, chunks))] if chunks > 1 else [[0]]
    pieces, ids = [], []
    for bundle in bundles:
        joined = jnp.concatenate([peaks[c] for c in bundle], 0) if len(bundle) > 1 else peaks[bundle[0]]
        pieces.append(gather_rows(joined, owners))
        local = np.concatenate([c * per_chunk + np.arange(per_chunk) for c in bundle])
        ids.append((np.asarray(order)[:, None] * gauges_here + local[None, :]).reshape(-1))
    gauge_ids = jnp.asarray(np.concatenate(ids).astype(np.int32))

    tile_total = coast_gauges.shape[0]
    slot_count = coast_gauges.shape[1]
    tiles_here = tile_total // owners
    active_slot = jnp.arange(slot_count, dtype=jnp.int32)[None, :] < coast_counts[:, None]
    weights = jnp.where(active_slot, coast_amps, jnp.zeros_like(coast_amps))
    first_tile = lax.axis_index("rows") * tiles_here
    mine_gauges = lax.dynamic_slice_in_dim(coast_gauges, first_tile, tiles_here, 0)
    mine_weights = lax.dynamic_slice_in_dim(weights, first_tile, tiles_here, 0)
    matches = mine_gauges[:, :, None] == gauge_ids[None, None, :]
    tile_table = jnp.sum(jnp.where(matches, mine_weights[:, :, None], 0.0), axis=1)
    onshore = None
    start = 0
    for piece in pieces:
        span = piece.shape[0]
        term = lax.dot_general(
            piece,
            tile_table[:, start:start + span],
            (((0,), (1,)), ((), ())),
            precision=lax.Precision.HIGHEST,
            preferred_element_type=jnp.float32,
        )
        start += span
        onshore = term if onshore is None else onshore + term
    return onshore


def solution(mesh):
    in_specs = (P(None, "src"), P(None, "src"), P("src", "rows"), P(), P(), P())
    out_specs = P("src", "rows")
    return jax.shard_map(body, mesh=mesh, in_specs=in_specs, out_specs=out_specs, check_vma=False)
```

```python
import functools

import numpy as np
import jax
import jax.numpy as jnp
from jax import lax
from jax.experimental import pallas as pl
from jax.experimental.pallas import tpu as pltpu
from jax.sharding import PartitionSpec as P

NT = 240
UBLK = 125
SEG = 1920


def matmul_kernel(slip_ref, green_ref, other_ref, mine_ref):
    half = other_ref.shape[1]
    product = lax.dot_general(
        green_ref[...], slip_ref[...], (((0,), (0,)), ((), ())), preferred_element_type=jnp.float32
    )
    other_ref[...] = product[:, :half].astype(jnp.bfloat16)
    mine_ref[...] = product[:, half:].astype(jnp.bfloat16)


def partials_of(slip_ordered, green, first, steps):
    sources, scenarios = slip_ordered.shape
    half = scenarios // 2
    tile = SEG
    width = steps * tile
    return pl.pallas_call(
        matmul_kernel,
        grid=(steps,),
        in_specs=[
            pl.BlockSpec((sources, scenarios), lambda j: (0, 0)),
            pl.BlockSpec((sources, tile), lambda j: (0, first + j)),
        ],
        out_specs=[pl.BlockSpec((tile, half), lambda j: (j, 0))] * 2,
        out_shape=[jax.ShapeDtypeStruct((width, half), jnp.bfloat16)] * 2,
        cost_estimate=pl.CostEstimate(
            flops=2 * scenarios * sources * width,
            transcendentals=0,
            bytes_accessed=2 * (sources * width + scenarios * width),
        ),
    )(slip_ordered, green)


def peak_kernel(mine_ref, recv_ref, out_ref):
    wave = mine_ref[...].astype(jnp.float32) + recv_ref[...].astype(jnp.float32)
    gauges = SEG // NT
    out_ref[...] = jnp.max(jnp.abs(wave).reshape(gauges, NT, wave.shape[1]), axis=1)


def fused_kernel(slip_ref, green_ref, mine_prev_ref, recv_prev_ref, other_ref, mine_ref, peaks_ref, *, steps, trail):
    j = pl.program_id(0)

    @pl.when(j < steps)
    def _():
        matmul_kernel(slip_ref, green_ref, other_ref, mine_ref)

    @pl.when(j < trail)
    def _():
        peak_kernel(mine_prev_ref, recv_prev_ref, peaks_ref)


def fused_of(slip_ordered, green, first, steps, mine_prev, recv_prev):
    sources, scenarios = slip_ordered.shape
    half = scenarios // 2
    trail = mine_prev.shape[0] // SEG
    gauges = SEG // NT
    here = lambda j: (jnp.minimum(j, steps - 1), 0)
    back = lambda j: (jnp.minimum(j, trail - 1), 0)
    return pl.pallas_call(
        functools.partial(fused_kernel, steps=steps, trail=trail),
        grid=(max(steps, trail),),
        in_specs=[
            pl.BlockSpec((sources, scenarios), lambda j: (0, 0)),
            pl.BlockSpec((sources, SEG), lambda j: (0, first + jnp.minimum(j, steps - 1))),
            pl.BlockSpec((SEG, half), back),
            pl.BlockSpec((SEG, half), back),
        ],
        out_specs=[
            pl.BlockSpec((SEG, half), here),
            pl.BlockSpec((SEG, half), here),
            pl.BlockSpec((gauges, half), back),
        ],
        out_shape=[
            jax.ShapeDtypeStruct((steps * SEG, half), jnp.bfloat16),
            jax.ShapeDtypeStruct((steps * SEG, half), jnp.bfloat16),
            jax.ShapeDtypeStruct((trail * gauges, half), jnp.float32),
        ],
        cost_estimate=pl.CostEstimate(
            flops=2 * scenarios * sources * steps * SEG,
            transcendentals=0,
            bytes_accessed=2 * (sources * steps * SEG + scenarios * (steps + trail) * SEG),
        ),
    )(slip_ordered, green, mine_prev, recv_prev)


def peaks_of(mine, recv):
    cols, rows = mine.shape
    blocks = cols // SEG
    gauges = SEG // NT
    return pl.pallas_call(
        peak_kernel,
        grid=(blocks,),
        in_specs=[pl.BlockSpec((SEG, rows), lambda j: (j, 0))] * 2,
        out_specs=pl.BlockSpec((gauges, rows), lambda j: (j, 0)),
        out_shape=jax.ShapeDtypeStruct((blocks * gauges, rows), jnp.float32),
        cost_estimate=pl.CostEstimate(
            flops=3 * rows * cols, transcendentals=0, bytes_accessed=4 * rows * cols
        ),
    )(mine, recv)


def chunk_plan(segments):
    if segments >= 8 and segments % 4 == 0:
        size = segments // 4
        return [size] * 3 + [size // 2, size - size // 2]
    return [1] * segments


def doubling_masks(owners):
    masks = []
    m = 1
    while m < owners:
        masks.append(m)
        m *= 2
    return masks[::-1]


def gather_rows(block, owners):
    me = lax.axis_index("rows")
    held = block.astype(jnp.bfloat16)
    for m in doubling_masks(owners):
        pairs = [(i, i ^ m) for i in range(owners)]
        got = lax.ppermute(held, "rows", pairs)
        upper = (me & m) != 0
        held = jnp.where(
            upper, jnp.concatenate([got, held], 0), jnp.concatenate([held, got], 0)
        )
    return held.astype(jnp.float32)


def arrival_order(owners):
    order = [0]
    for m in doubling_masks(owners):
        order = order + [d ^ m for d in order]
    return order


def body(slip_units, slip_scales, green, coast_gauges, coast_amps, coast_counts):
    scenarios = slip_units.shape[0]
    units_t = slip_units.T.astype(jnp.float32)
    scale_rows = jnp.repeat(slip_scales.T, UBLK, axis=0)
    slip_t = (units_t * scale_rows).astype(jnp.bfloat16)
    me = lax.axis_index("src")
    groups = lax.axis_size("src")
    portion = scenarios // groups
    slip_mine = lax.dynamic_slice_in_dim(slip_t, me * portion, portion, 1)
    slip_other = lax.dynamic_slice_in_dim(slip_t, (1 - me) * portion, portion, 1)
    slip_ordered = jnp.concatenate([slip_other, slip_mine], 1)
    pairs = [(0, 1), (1, 0)]

    owners = lax.axis_size("rows")
    columns = green.shape[1]
    gauges_here = columns // NT
    segments = columns // SEG
    sizes = chunk_plan(segments)
    chunks = len(sizes)
    firsts = [sum(sizes[:c]) for c in range(chunks)]
    gauges_per_seg = SEG // NT
    order = arrival_order(owners)
    mines, receiveds, peaks = [], [], [None] * chunks
    for c in range(chunks):
        if c >= 2 and sizes[c] >= 2:
            other, mine, peaks[c - 2] = fused_of(
                slip_ordered, green, firsts[c], sizes[c], mines[c - 2], receiveds[c - 2]
            )
        else:
            other, mine = partials_of(slip_ordered, green, firsts[c], sizes[c])
        mines.append(mine)
        receiveds.append(lax.ppermute(other, "src", pairs))
    for c in range(chunks):
        if peaks[c] is None:
            peaks[c] = peaks_of(mines[c], receiveds[c])
    tail = 2 if chunks > 2 else chunks
    bundles = [list(range(chunks - tail)), list(range(chunks - tail, chunks))] if chunks > tail else [list(range(chunks))]
    pieces, ids = [], []
    for bundle in bundles:
        joined = jnp.concatenate([peaks[c] for c in bundle], 0) if len(bundle) > 1 else peaks[bundle[0]]
        pieces.append(gather_rows(joined, owners))
        local = np.concatenate(
            [firsts[c] * gauges_per_seg + np.arange(sizes[c] * gauges_per_seg) for c in bundle]
        )
        ids.append((np.asarray(order)[:, None] * gauges_here + local[None, :]).reshape(-1))
    gauge_ids = jnp.asarray(np.concatenate(ids).astype(np.int32))

    tile_total = coast_gauges.shape[0]
    slot_count = coast_gauges.shape[1]
    tiles_here = tile_total // owners
    active_slot = jnp.arange(slot_count, dtype=jnp.int32)[None, :] < coast_counts[:, None]
    weights = jnp.where(active_slot, coast_amps, jnp.zeros_like(coast_amps))
    first_tile = lax.axis_index("rows") * tiles_here
    mine_gauges = lax.dynamic_slice_in_dim(coast_gauges, first_tile, tiles_here, 0)
    mine_weights = lax.dynamic_slice_in_dim(weights, first_tile, tiles_here, 0)
    matches = mine_gauges[:, :, None] == gauge_ids[None, None, :]
    tile_table = jnp.sum(jnp.where(matches, mine_weights[:, :, None], 0.0), axis=1)
    onshore = None
    start = 0
    for piece in pieces:
        span = piece.shape[0]
        term = lax.dot_general(
            piece,
            tile_table[:, start:start + span],
            (((0,), (1,)), ((), ())),
            precision=lax.Precision.HIGHEST,
            preferred_element_type=jnp.float32,
        )
        start += span
        onshore = term if onshore is None else onshore + term
    return onshore


def solution(mesh):
    in_specs = (P(None, "src"), P(None, "src"), P("src", "rows"), P(), P(), P())
    out_specs = P("src", "rows")
    return jax.shard_map(body, mesh=mesh, in_specs=in_specs, out_specs=out_specs, check_vma=False)
```

```python
import numpy as np
import jax
import jax.numpy as jnp
from jax import lax
from jax.experimental import pallas as pl
from jax.experimental.pallas import tpu as pltpu
from jax.sharding import PartitionSpec as P

NT = 240
UBLK = 125
SEG = 1920


def matmul_kernel(slip_ref, green_ref, other_ref, mine_ref):
    half = other_ref.shape[1]
    product = lax.dot_general(
        green_ref[...], slip_ref[...], (((0,), (0,)), ((), ())), preferred_element_type=jnp.float32
    )
    other_ref[...] = product[:, :half].astype(jnp.bfloat16)
    mine_ref[...] = product[:, half:].astype(jnp.bfloat16)


def partials_of(slip_ordered, green, chunk, width, tile):
    sources, scenarios = slip_ordered.shape
    half = scenarios // 2
    steps = width // tile
    return pl.pallas_call(
        matmul_kernel,
        grid=(steps,),
        in_specs=[
            pl.BlockSpec((sources, scenarios), lambda j: (0, 0)),
            pl.BlockSpec((sources, tile), lambda j: (0, chunk * steps + j)),
        ],
        out_specs=[pl.BlockSpec((tile, half), lambda j: (j, 0))] * 2,
        out_shape=[jax.ShapeDtypeStruct((width, half), jnp.bfloat16)] * 2,
        cost_estimate=pl.CostEstimate(
            flops=2 * scenarios * sources * width,
            transcendentals=0,
            bytes_accessed=2 * (sources * width + scenarios * width),
        ),
    )(slip_ordered, green)


def peak_kernel(mine_ref, recv_ref, out_ref):
    wave = mine_ref[...].astype(jnp.float32) + recv_ref[...].astype(jnp.float32)
    gauges = SEG // NT
    out_ref[...] = jnp.max(jnp.abs(wave).reshape(gauges, NT, wave.shape[1]), axis=1)


def fused_kernel(slip_ref, green_ref, mine_prev_ref, recv_prev_ref, other_ref, mine_ref, peaks_ref):
    matmul_kernel(slip_ref, green_ref, other_ref, mine_ref)
    peak_kernel(mine_prev_ref, recv_prev_ref, peaks_ref)


def fused_of(slip_ordered, green, chunk, width, mine_prev, recv_prev):
    sources, scenarios = slip_ordered.shape
    half = scenarios // 2
    steps = width // SEG
    gauges = SEG // NT
    return pl.pallas_call(
        fused_kernel,
        grid=(steps,),
        in_specs=[
            pl.BlockSpec((sources, scenarios), lambda j: (0, 0)),
            pl.BlockSpec((sources, SEG), lambda j: (0, chunk * steps + j)),
            pl.BlockSpec((SEG, half), lambda j: (j, 0)),
            pl.BlockSpec((SEG, half), lambda j: (j, 0)),
        ],
        out_specs=[
            pl.BlockSpec((SEG, half), lambda j: (j, 0)),
            pl.BlockSpec((SEG, half), lambda j: (j, 0)),
            pl.BlockSpec((gauges, half), lambda j: (j, 0)),
        ],
        out_shape=[
            jax.ShapeDtypeStruct((width, half), jnp.bfloat16),
            jax.ShapeDtypeStruct((width, half), jnp.bfloat16),
            jax.ShapeDtypeStruct((steps * gauges, half), jnp.float32),
        ],
        cost_estimate=pl.CostEstimate(
            flops=2 * scenarios * sources * width,
            transcendentals=0,
            bytes_accessed=2 * (sources * width + 2 * scenarios * width),
        ),
    )(slip_ordered, green, mine_prev, recv_prev)


def peaks_of(mine, recv):
    cols, rows = mine.shape
    blocks = cols // SEG
    gauges = SEG // NT
    return pl.pallas_call(
        peak_kernel,
        grid=(blocks,),
        in_specs=[pl.BlockSpec((SEG, rows), lambda j: (j, 0))] * 2,
        out_specs=pl.BlockSpec((gauges, rows), lambda j: (j, 0)),
        out_shape=jax.ShapeDtypeStruct((blocks * gauges, rows), jnp.float32),
        cost_estimate=pl.CostEstimate(
            flops=3 * rows * cols, transcendentals=0, bytes_accessed=4 * rows * cols
        ),
    )(mine, recv)


def doubling_masks(owners):
    masks = []
    m = 1
    while m < owners:
        masks.append(m)
        m *= 2
    return masks[::-1]


def gather_rows(block, owners):
    me = lax.axis_index("rows")
    held = block.astype(jnp.bfloat16)
    for m in doubling_masks(owners):
        pairs = [(i, i ^ m) for i in range(owners)]
        got = lax.ppermute(held, "rows", pairs)
        upper = (me & m) != 0
        held = jnp.where(
            upper, jnp.concatenate([got, held], 0), jnp.concatenate([held, got], 0)
        )
    return held.astype(jnp.float32)


def arrival_order(owners):
    order = [0]
    for m in doubling_masks(owners):
        order = order + [d ^ m for d in order]
    return order


def body(slip_units, slip_scales, green, coast_gauges, coast_amps, coast_counts):
    scenarios = slip_units.shape[0]
    units_t = slip_units.T.astype(jnp.float32)
    block_of = jnp.arange(slip_units.shape[1], dtype=jnp.int32) // UBLK
    picks = (block_of[:, None] == jnp.arange(slip_scales.shape[1], dtype=jnp.int32)[None, :]).astype(jnp.float32)
    scale_rows = jnp.dot(picks, slip_scales.T, precision=lax.Precision.HIGHEST, preferred_element_type=jnp.float32)
    slip_t = (units_t * scale_rows).astype(jnp.bfloat16)
    me = lax.axis_index("src")
    groups = lax.axis_size("src")
    portion = scenarios // groups
    slip_mine = lax.dynamic_slice_in_dim(slip_t, me * portion, portion, 1)
    slip_other = lax.dynamic_slice_in_dim(slip_t, (1 - me) * portion, portion, 1)
    slip_ordered = jnp.concatenate([slip_other, slip_mine], 1)
    pairs = [(0, 1), (1, 0)]

    owners = lax.axis_size("rows")
    columns = green.shape[1]
    gauges_here = columns // NT
    segments = columns // SEG
    chunks = max(c for c in (1, 2, 4) if segments % c == 0)
    width = columns // chunks
    tile = SEG
    per_chunk = gauges_here // chunks
    order = arrival_order(owners)
    lag = 2 if chunks > 2 else 0
    mines, receiveds, peaks = [], [], [None] * chunks
    for c in range(chunks):
        if lag and c >= lag:
            other, mine, peaks[c - lag] = fused_of(
                slip_ordered, green, c, width, mines[c - lag], receiveds[c - lag]
            )
        else:
            other, mine = partials_of(slip_ordered, green, c, width, tile)
        mines.append(mine)
        receiveds.append(lax.ppermute(other, "src", pairs))
    for c in range(chunks):
        if peaks[c] is None:
            peaks[c] = peaks_of(mines[c], receiveds[c])
    split = (chunks + 1) // 2
    bundles = [list(range(split)), list(range(split, chunks))] if chunks > 1 else [[0]]
    pieces, ids = [], []
    for bundle in bundles:
        joined = jnp.concatenate([peaks[c] for c in bundle], 0) if len(bundle) > 1 else peaks[bundle[0]]
        pieces.append(gather_rows(joined, owners))
        local = np.concatenate([c * per_chunk + np.arange(per_chunk) for c in bundle])
        ids.append((np.asarray(order)[:, None] * gauges_here + local[None, :]).reshape(-1))
    gauge_ids = jnp.asarray(np.concatenate(ids).astype(np.int32))

    tile_total = coast_gauges.shape[0]
    slot_count = coast_gauges.shape[1]
    tiles_here = tile_total // owners
    active_slot = jnp.arange(slot_count, dtype=jnp.int32)[None, :] < coast_counts[:, None]
    weights = jnp.where(active_slot, coast_amps, jnp.zeros_like(coast_amps))
    first_tile = lax.axis_index("rows") * tiles_here
    mine_gauges = lax.dynamic_slice_in_dim(coast_gauges, first_tile, tiles_here, 0)
    mine_weights = lax.dynamic_slice_in_dim(weights, first_tile, tiles_here, 0)
    matches = mine_gauges[:, :, None] == gauge_ids[None, None, :]
    tile_table = jnp.sum(jnp.where(matches, mine_weights[:, :, None], 0.0), axis=1)
    onshore = None
    start = 0
    for piece in pieces:
        span = piece.shape[0]
        term = lax.dot_general(
            piece,
            tile_table[:, start:start + span],
            (((0,), (1,)), ((), ())),
            precision=lax.Precision.HIGHEST,
            preferred_element_type=jnp.float32,
        )
        start += span
        onshore = term if onshore is None else onshore + term
    return onshore


def solution(mesh):
    in_specs = (P(None, "src"), P(None, "src"), P("src", "rows"), P(), P(), P())
    out_specs = P("src", "rows")
    return jax.shard_map(body, mesh=mesh, in_specs=in_specs, out_specs=out_specs, check_vma=False)
```

```python
import numpy as np
import jax
import jax.numpy as jnp
from jax import lax
from jax.experimental import pallas as pl
from jax.experimental.pallas import tpu as pltpu
from jax.sharding import PartitionSpec as P

NT = 240
UBLK = 125
SEG = 1920


def matmul_kernel(slip_ref, green_ref, other_ref, mine_ref):
    half = other_ref.shape[1]
    product = lax.dot_general(
        green_ref[...], slip_ref[...], (((0,), (0,)), ((), ())), preferred_element_type=jnp.float32
    )
    other_ref[...] = product[:, :half].astype(jnp.bfloat16)
    mine_ref[...] = product[:, half:].astype(jnp.bfloat16)


def partials_of(slip_ordered, green, chunk, width, tile):
    sources, scenarios = slip_ordered.shape
    half = scenarios // 2
    steps = width // tile
    return pl.pallas_call(
        matmul_kernel,
        grid=(steps,),
        in_specs=[
            pl.BlockSpec((sources, scenarios), lambda j: (0, 0)),
            pl.BlockSpec((sources, tile), lambda j: (0, chunk * steps + j)),
        ],
        out_specs=[pl.BlockSpec((tile, half), lambda j: (j, 0))] * 2,
        out_shape=[jax.ShapeDtypeStruct((width, half), jnp.bfloat16)] * 2,
        cost_estimate=pl.CostEstimate(
            flops=2 * scenarios * sources * width,
            transcendentals=0,
            bytes_accessed=2 * (sources * width + scenarios * width),
        ),
    )(slip_ordered, green)


def peak_kernel(mine_ref, recv_ref, out_ref):
    wave = mine_ref[...].astype(jnp.float32) + recv_ref[...].astype(jnp.float32)
    gauges = SEG // NT
    out_ref[...] = jnp.max(jnp.abs(wave).reshape(gauges, NT, wave.shape[1]), axis=1)


def fused_kernel(slip_ref, green_ref, mine_prev_ref, recv_prev_ref, other_ref, mine_ref, peaks_ref):
    matmul_kernel(slip_ref, green_ref, other_ref, mine_ref)
    peak_kernel(mine_prev_ref, recv_prev_ref, peaks_ref)


def fused_of(slip_ordered, green, chunk, width, mine_prev, recv_prev):
    sources, scenarios = slip_ordered.shape
    half = scenarios // 2
    steps = width // SEG
    gauges = SEG // NT
    return pl.pallas_call(
        fused_kernel,
        grid=(steps,),
        in_specs=[
            pl.BlockSpec((sources, scenarios), lambda j: (0, 0)),
            pl.BlockSpec((sources, SEG), lambda j: (0, chunk * steps + j)),
            pl.BlockSpec((SEG, half), lambda j: (j, 0)),
            pl.BlockSpec((SEG, half), lambda j: (j, 0)),
        ],
        out_specs=[
            pl.BlockSpec((SEG, half), lambda j: (j, 0)),
            pl.BlockSpec((SEG, half), lambda j: (j, 0)),
            pl.BlockSpec((gauges, half), lambda j: (j, 0)),
        ],
        out_shape=[
            jax.ShapeDtypeStruct((width, half), jnp.bfloat16),
            jax.ShapeDtypeStruct((width, half), jnp.bfloat16),
            jax.ShapeDtypeStruct((steps * gauges, half), jnp.float32),
        ],
        cost_estimate=pl.CostEstimate(
            flops=2 * scenarios * sources * width,
            transcendentals=0,
            bytes_accessed=2 * (sources * width + 2 * scenarios * width),
        ),
    )(slip_ordered, green, mine_prev, recv_prev)


def peaks_of(mine, recv):
    cols, rows = mine.shape
    blocks = cols // SEG
    gauges = SEG // NT
    return pl.pallas_call(
        peak_kernel,
        grid=(blocks,),
        in_specs=[pl.BlockSpec((SEG, rows), lambda j: (j, 0))] * 2,
        out_specs=pl.BlockSpec((gauges, rows), lambda j: (j, 0)),
        out_shape=jax.ShapeDtypeStruct((blocks * gauges, rows), jnp.float32),
        cost_estimate=pl.CostEstimate(
            flops=3 * rows * cols, transcendentals=0, bytes_accessed=4 * rows * cols
        ),
    )(mine, recv)


def doubling_masks(owners):
    masks = []
    m = 1
    while m < owners:
        masks.append(m)
        m *= 2
    return masks[::-1]


def gather_rows(block, owners, ties=()):
    me = lax.axis_index("rows")
    held = block.astype(jnp.bfloat16)
    tied = []
    for i, m in enumerate(doubling_masks(owners)):
        if 1 <= i <= len(ties):
            held, value = lax.optimization_barrier((held, ties[i - 1]))
            tied.append(value)
        pairs = [(k, k ^ m) for k in range(owners)]
        got = lax.ppermute(held, "rows", pairs)
        upper = (me & m) != 0
        held = jnp.where(
            upper, jnp.concatenate([got, held], 0), jnp.concatenate([held, got], 0)
        )
    return held.astype(jnp.float32), tied + list(ties[len(tied):])


def arrival_order(owners):
    order = [0]
    for m in doubling_masks(owners):
        order = order + [d ^ m for d in order]
    return order


def body(slip_units, slip_scales, green, coast_gauges, coast_amps, coast_counts):
    scenarios = slip_units.shape[0]
    units_t = slip_units.T.astype(jnp.float32)
    block_of = jnp.arange(slip_units.shape[1], dtype=jnp.int32) // UBLK
    picks = (block_of[:, None] == jnp.arange(slip_scales.shape[1], dtype=jnp.int32)[None, :]).astype(jnp.float32)
    scale_rows = jnp.dot(picks, slip_scales.T, precision=lax.Precision.HIGHEST, preferred_element_type=jnp.float32)
    slip_t = (units_t * scale_rows).astype(jnp.bfloat16)
    me = lax.axis_index("src")
    groups = lax.axis_size("src")
    portion = scenarios // groups
    slip_mine = lax.dynamic_slice_in_dim(slip_t, me * portion, portion, 1)
    slip_other = lax.dynamic_slice_in_dim(slip_t, (1 - me) * portion, portion, 1)
    slip_ordered = jnp.concatenate([slip_other, slip_mine], 1)
    pairs = [(0, 1), (1, 0)]

    owners = lax.axis_size("rows")
    columns = green.shape[1]
    gauges_here = columns // NT
    segments = columns // SEG
    chunks = max(c for c in (1, 2, 4) if segments % c == 0)
    width = columns // chunks
    tile = SEG
    per_chunk = gauges_here // chunks
    order = arrival_order(owners)
    lag = 2 if chunks > 2 else 0
    mines, receiveds, peaks = [], [], [None] * chunks
    for c in range(chunks):
        if lag and c >= lag:
            other, mine, peaks[c - lag] = fused_of(
                slip_ordered, green, c, width, mines[c - lag], receiveds[c - lag]
            )
        else:
            other, mine = partials_of(slip_ordered, green, c, width, tile)
        mines.append(mine)
        receiveds.append(lax.ppermute(other, "src", pairs))
    waiting = [c for c in range(chunks) if peaks[c] is None]
    for c in waiting:
        peaks[c] = peaks_of(mines[c], receiveds[c])
    split = (chunks + 1) // 2
    bundles = [list(range(split)), list(range(split, chunks))] if chunks > 1 else [[0]]
    pieces, ids = [], []
    for b, bundle in enumerate(bundles):
        joined = jnp.concatenate([peaks[c] for c in bundle], 0) if len(bundle) > 1 else peaks[bundle[0]]
        ties = [peaks[c] for c in waiting if c not in bundle] if b == 0 else []
        piece, tied = gather_rows(joined, owners, ties)
        for c, value in zip([c for c in waiting if c not in bundle] if b == 0 else [], tied):
            peaks[c] = value
        pieces.append(piece)
        local = np.concatenate([c * per_chunk + np.arange(per_chunk) for c in bundle])
        ids.append((np.asarray(order)[:, None] * gauges_here + local[None, :]).reshape(-1))
    gauge_ids = jnp.asarray(np.concatenate(ids).astype(np.int32))

    tile_total = coast_gauges.shape[0]
    slot_count = coast_gauges.shape[1]
    tiles_here = tile_total // owners
    active_slot = jnp.arange(slot_count, dtype=jnp.int32)[None, :] < coast_counts[:, None]
    weights = jnp.where(active_slot, coast_amps, jnp.zeros_like(coast_amps))
    first_tile = lax.axis_index("rows") * tiles_here
    mine_gauges = lax.dynamic_slice_in_dim(coast_gauges, first_tile, tiles_here, 0)
    mine_weights = lax.dynamic_slice_in_dim(weights, first_tile, tiles_here, 0)
    matches = mine_gauges[:, :, None] == gauge_ids[None, None, :]
    tile_table = jnp.sum(jnp.where(matches, mine_weights[:, :, None], 0.0), axis=1)
    onshore = None
    start = 0
    for piece in pieces:
        span = piece.shape[0]
        term = lax.dot_general(
            piece,
            tile_table[:, start:start + span],
            (((0,), (1,)), ((), ())),
            precision=lax.Precision.HIGHEST,
            preferred_element_type=jnp.float32,
        )
        start += span
        onshore = term if onshore is None else onshore + term
    return onshore


def solution(mesh):
    in_specs = (P(None, "src"), P(None, "src"), P("src", "rows"), P(), P(), P())
    out_specs = P("src", "rows")
    return jax.shard_map(body, mesh=mesh, in_specs=in_specs, out_specs=out_specs, check_vma=False)
```

```python
import numpy as np
import jax
import jax.numpy as jnp
from jax import lax
from jax.experimental import pallas as pl
from jax.experimental.pallas import tpu as pltpu
from jax.sharding import PartitionSpec as P

NT = 240
UBLK = 125
SEG = 1920


def matmul_kernel(side_ref, other_slip_ref, mine_slip_ref, green_ref, other_ref, mine_ref):
    block = green_ref[...]
    for slip_ref, out_ref in ((other_slip_ref, other_ref), (mine_slip_ref, mine_ref)):
        product = lax.dot_general(
            block, slip_ref[...], (((0,), (0,)), ((), ())), preferred_element_type=jnp.float32
        )
        out_ref[...] = product.astype(jnp.bfloat16)


def slip_specs(sources, half):
    return [
        pl.BlockSpec((sources, half), lambda j, side: (0, 1 - side[0])),
        pl.BlockSpec((sources, half), lambda j, side: (0, side[0])),
    ]


def partials_of(side, slip_t, green, chunk, width, tile):
    sources, scenarios = slip_t.shape
    half = scenarios // 2
    steps = width // tile
    return pl.pallas_call(
        matmul_kernel,
        grid_spec=pltpu.PrefetchScalarGridSpec(
            num_scalar_prefetch=1,
            grid=(steps,),
            in_specs=slip_specs(sources, half)
            + [pl.BlockSpec((sources, tile), lambda j, side: (0, chunk * steps + j))],
            out_specs=[pl.BlockSpec((tile, half), lambda j, side: (j, 0))] * 2,
        ),
        out_shape=[jax.ShapeDtypeStruct((width, half), jnp.bfloat16)] * 2,
        cost_estimate=pl.CostEstimate(
            flops=2 * scenarios * sources * width,
            transcendentals=0,
            bytes_accessed=2 * (sources * width + scenarios * width),
        ),
    )(side, slip_t, slip_t, green)


def peak_kernel(mine_ref, recv_ref, out_ref):
    wave = mine_ref[...].astype(jnp.float32) + recv_ref[...].astype(jnp.float32)
    gauges = SEG // NT
    out_ref[...] = jnp.max(jnp.abs(wave).reshape(gauges, NT, wave.shape[1]), axis=1)


def fused_kernel(side_ref, other_slip_ref, mine_slip_ref, green_ref, mine_prev_ref, recv_prev_ref, other_ref, mine_ref, peaks_ref):
    matmul_kernel(side_ref, other_slip_ref, mine_slip_ref, green_ref, other_ref, mine_ref)
    peak_kernel(mine_prev_ref, recv_prev_ref, peaks_ref)


def fused_of(side, slip_t, green, chunk, width, mine_prev, recv_prev):
    sources, scenarios = slip_t.shape
    half = scenarios // 2
    steps = width // SEG
    gauges = SEG // NT
    return pl.pallas_call(
        fused_kernel,
        grid_spec=pltpu.PrefetchScalarGridSpec(
            num_scalar_prefetch=1,
            grid=(steps,),
            in_specs=slip_specs(sources, half)
            + [
                pl.BlockSpec((sources, SEG), lambda j, side: (0, chunk * steps + j)),
                pl.BlockSpec((SEG, half), lambda j, side: (j, 0)),
                pl.BlockSpec((SEG, half), lambda j, side: (j, 0)),
            ],
            out_specs=[
                pl.BlockSpec((SEG, half), lambda j, side: (j, 0)),
                pl.BlockSpec((SEG, half), lambda j, side: (j, 0)),
                pl.BlockSpec((gauges, half), lambda j, side: (j, 0)),
            ],
        ),
        out_shape=[
            jax.ShapeDtypeStruct((width, half), jnp.bfloat16),
            jax.ShapeDtypeStruct((width, half), jnp.bfloat16),
            jax.ShapeDtypeStruct((steps * gauges, half), jnp.float32),
        ],
        cost_estimate=pl.CostEstimate(
            flops=2 * scenarios * sources * width,
            transcendentals=0,
            bytes_accessed=2 * (sources * width + 2 * scenarios * width),
        ),
    )(side, slip_t, slip_t, green, mine_prev, recv_prev)


def peaks_of(mine, recv):
    cols, rows = mine.shape
    blocks = cols // SEG
    gauges = SEG // NT
    return pl.pallas_call(
        peak_kernel,
        grid=(blocks,),
        in_specs=[pl.BlockSpec((SEG, rows), lambda j: (j, 0))] * 2,
        out_specs=pl.BlockSpec((gauges, rows), lambda j: (j, 0)),
        out_shape=jax.ShapeDtypeStruct((blocks * gauges, rows), jnp.float32),
        cost_estimate=pl.CostEstimate(
            flops=3 * rows * cols, transcendentals=0, bytes_accessed=4 * rows * cols
        ),
    )(mine, recv)


def doubling_masks(owners):
    masks = []
    m = 1
    while m < owners:
        masks.append(m)
        m *= 2
    return masks[::-1]


def gather_rows(block, owners):
    me = lax.axis_index("rows")
    held = block.astype(jnp.bfloat16)
    for m in doubling_masks(owners):
        pairs = [(i, i ^ m) for i in range(owners)]
        got = lax.ppermute(held, "rows", pairs)
        upper = (me & m) != 0
        held = jnp.where(
            upper, jnp.concatenate([got, held], 0), jnp.concatenate([held, got], 0)
        )
    return held.astype(jnp.float32)


def arrival_order(owners):
    order = [0]
    for m in doubling_masks(owners):
        order = order + [d ^ m for d in order]
    return order


def body(slip_units, slip_scales, green, coast_gauges, coast_amps, coast_counts):
    scenarios = slip_units.shape[0]
    units_t = slip_units.T.astype(jnp.float32)
    block_of = jnp.arange(slip_units.shape[1], dtype=jnp.int32) // UBLK
    picks = (block_of[:, None] == jnp.arange(slip_scales.shape[1], dtype=jnp.int32)[None, :]).astype(jnp.float32)
    scale_rows = jnp.dot(picks, slip_scales.T, precision=lax.Precision.HIGHEST, preferred_element_type=jnp.float32)
    slip_t = (units_t * scale_rows).astype(jnp.bfloat16)
    me = lax.axis_index("src")
    groups = lax.axis_size("src")
    portion = scenarios // groups
    side = jnp.reshape(me, (1,)).astype(jnp.int32)
    pairs = [(0, 1), (1, 0)]

    owners = lax.axis_size("rows")
    columns = green.shape[1]
    gauges_here = columns // NT
    segments = columns // SEG
    chunks = max(c for c in (1, 2, 4) if segments % c == 0)
    width = columns // chunks
    tile = SEG
    per_chunk = gauges_here // chunks
    order = arrival_order(owners)
    lag = 2 if chunks > 2 else 0
    mines, receiveds, peaks = [], [], [None] * chunks
    for c in range(chunks):
        if lag and c >= lag:
            other, mine, peaks[c - lag] = fused_of(
                side, slip_t, green, c, width, mines[c - lag], receiveds[c - lag]
            )
        else:
            other, mine = partials_of(side, slip_t, green, c, width, tile)
        mines.append(mine)
        receiveds.append(lax.ppermute(other, "src", pairs))
    for c in range(chunks):
        if peaks[c] is None:
            peaks[c] = peaks_of(mines[c], receiveds[c])
    split = (chunks + 1) // 2
    bundles = [list(range(split)), list(range(split, chunks))] if chunks > 1 else [[0]]
    pieces, ids = [], []
    for bundle in bundles:
        joined = jnp.concatenate([peaks[c] for c in bundle], 0) if len(bundle) > 1 else peaks[bundle[0]]
        pieces.append(gather_rows(joined, owners))
        local = np.concatenate([c * per_chunk + np.arange(per_chunk) for c in bundle])
        ids.append((np.asarray(order)[:, None] * gauges_here + local[None, :]).reshape(-1))
    gauge_ids = jnp.asarray(np.concatenate(ids).astype(np.int32))

    tile_total = coast_gauges.shape[0]
    slot_count = coast_gauges.shape[1]
    tiles_here = tile_total // owners
    active_slot = jnp.arange(slot_count, dtype=jnp.int32)[None, :] < coast_counts[:, None]
    weights = jnp.where(active_slot, coast_amps, jnp.zeros_like(coast_amps))
    first_tile = lax.axis_index("rows") * tiles_here
    mine_gauges = lax.dynamic_slice_in_dim(coast_gauges, first_tile, tiles_here, 0)
    mine_weights = lax.dynamic_slice_in_dim(weights, first_tile, tiles_here, 0)
    matches = mine_gauges[:, :, None] == gauge_ids[None, None, :]
    tile_table = jnp.sum(jnp.where(matches, mine_weights[:, :, None], 0.0), axis=1)
    onshore = None
    start = 0
    for piece in pieces:
        span = piece.shape[0]
        term = lax.dot_general(
            piece,
            tile_table[:, start:start + span],
            (((0,), (1,)), ((), ())),
            precision=lax.Precision.HIGHEST,
            preferred_element_type=jnp.float32,
        )
        start += span
        onshore = term if onshore is None else onshore + term
    return onshore


def solution(mesh):
    in_specs = (P(None, "src"), P(None, "src"), P("src", "rows"), P(), P(), P())
    out_specs = P("src", "rows")
    return jax.shard_map(body, mesh=mesh, in_specs=in_specs, out_specs=out_specs, check_vma=False)
```

```python
import numpy as np
import jax
import jax.numpy as jnp
from jax import lax
from jax.experimental import pallas as pl
from jax.experimental.pallas import tpu as pltpu
from jax.sharding import PartitionSpec as P

NT = 240
UBLK = 125
SEG = 1920


def matmul_kernel(side_ref, other_slip_ref, mine_slip_ref, green_ref, other_ref, mine_ref):
    block = green_ref[...]
    for slip_ref, out_ref in ((other_slip_ref, other_ref), (mine_slip_ref, mine_ref)):
        product = lax.dot_general(
            block, slip_ref[...], (((0,), (0,)), ((), ())), preferred_element_type=jnp.float32
        )
        out_ref[...] = product.astype(jnp.bfloat16)


def slip_specs(sources, half):
    return [
        pl.BlockSpec((sources, half), lambda j, side: (0, 1 - side[0])),
        pl.BlockSpec((sources, half), lambda j, side: (0, side[0])),
    ]


def partials_of(side, slip_t, green, chunk, width, tile):
    sources, scenarios = slip_t.shape
    half = scenarios // 2
    steps = width // tile
    return pl.pallas_call(
        matmul_kernel,
        grid_spec=pltpu.PrefetchScalarGridSpec(
            num_scalar_prefetch=1,
            grid=(steps,),
            in_specs=slip_specs(sources, half)
            + [pl.BlockSpec((sources, tile), lambda j, side: (0, chunk * steps + j))],
            out_specs=[pl.BlockSpec((tile, half), lambda j, side: (j, 0))] * 2,
        ),
        out_shape=[jax.ShapeDtypeStruct((width, half), jnp.bfloat16)] * 2,
        cost_estimate=pl.CostEstimate(
            flops=2 * scenarios * sources * width,
            transcendentals=0,
            bytes_accessed=2 * (sources * width + scenarios * width),
        ),
    )(side, slip_t, slip_t, green)


def peak_kernel(mine_ref, recv_ref, out_ref):
    wave = mine_ref[...].astype(jnp.float32) + recv_ref[...].astype(jnp.float32)
    gauges = SEG // NT
    out_ref[...] = jnp.max(jnp.abs(wave).reshape(gauges, NT, wave.shape[1]), axis=1)


def fused_kernel(side_ref, other_slip_ref, mine_slip_ref, green_ref, mine_prev_ref, recv_prev_ref, other_ref, mine_ref, peaks_ref):
    matmul_kernel(side_ref, other_slip_ref, mine_slip_ref, green_ref, other_ref, mine_ref)
    peak_kernel(mine_prev_ref, recv_prev_ref, peaks_ref)


def fused_of(side, slip_t, green, chunk, width, mine_prev, recv_prev):
    sources, scenarios = slip_t.shape
    half = scenarios // 2
    steps = width // SEG
    gauges = SEG // NT
    return pl.pallas_call(
        fused_kernel,
        grid_spec=pltpu.PrefetchScalarGridSpec(
            num_scalar_prefetch=1,
            grid=(steps,),
            in_specs=slip_specs(sources, half)
            + [
                pl.BlockSpec((sources, SEG), lambda j, side: (0, chunk * steps + j)),
                pl.BlockSpec((SEG, half), lambda j, side: (j, 0)),
                pl.BlockSpec((SEG, half), lambda j, side: (j, 0)),
            ],
            out_specs=[
                pl.BlockSpec((SEG, half), lambda j, side: (j, 0)),
                pl.BlockSpec((SEG, half), lambda j, side: (j, 0)),
                pl.BlockSpec((gauges, half), lambda j, side: (j, 0)),
            ],
        ),
        out_shape=[
            jax.ShapeDtypeStruct((width, half), jnp.bfloat16),
            jax.ShapeDtypeStruct((width, half), jnp.bfloat16),
            jax.ShapeDtypeStruct((steps * gauges, half), jnp.float32),
        ],
        cost_estimate=pl.CostEstimate(
            flops=2 * scenarios * sources * width,
            transcendentals=0,
            bytes_accessed=2 * (sources * width + 2 * scenarios * width),
        ),
    )(side, slip_t, slip_t, green, mine_prev, recv_prev)


def peaks_of(mine, recv):
    cols, rows = mine.shape
    blocks = cols // SEG
    gauges = SEG // NT
    return pl.pallas_call(
        peak_kernel,
        grid=(blocks,),
        in_specs=[pl.BlockSpec((SEG, rows), lambda j: (j, 0))] * 2,
        out_specs=pl.BlockSpec((gauges, rows), lambda j: (j, 0)),
        out_shape=jax.ShapeDtypeStruct((blocks * gauges, rows), jnp.float32),
        cost_estimate=pl.CostEstimate(
            flops=3 * rows * cols, transcendentals=0, bytes_accessed=4 * rows * cols
        ),
    )(mine, recv)


def slip_kernel(units_ref, scales_ref, out_ref, acc_ref):
    for b in range(scales_ref.shape[0]):
        rows = pl.ds(b * UBLK, UBLK)
        acc_ref[rows, :] = units_ref[rows, :].astype(jnp.float32) * scales_ref[b:b + 1, :]
    out_ref[...] = acc_ref[...].astype(jnp.bfloat16)


def slip_of(units_t, scales_t):
    sources, scenarios = units_t.shape
    return pl.pallas_call(
        slip_kernel,
        out_shape=jax.ShapeDtypeStruct((sources, scenarios), jnp.bfloat16),
        scratch_shapes=[pltpu.VMEM((sources, scenarios), jnp.float32)],
    )(units_t, scales_t)


def doubling_masks(owners):
    masks = []
    m = 1
    while m < owners:
        masks.append(m)
        m *= 2
    return masks[::-1]


def gather_rows(block, owners):
    me = lax.axis_index("rows")
    held = block.astype(jnp.bfloat16)
    for m in doubling_masks(owners):
        pairs = [(i, i ^ m) for i in range(owners)]
        got = lax.ppermute(held, "rows", pairs)
        upper = (me & m) != 0
        held = jnp.where(
            upper, jnp.concatenate([got, held], 0), jnp.concatenate([held, got], 0)
        )
    return held.astype(jnp.float32)


def arrival_order(owners):
    order = [0]
    for m in doubling_masks(owners):
        order = order + [d ^ m for d in order]
    return order


def body(slip_units, slip_scales, green, coast_gauges, coast_amps, coast_counts):
    scenarios = slip_units.shape[0]
    slip_t = slip_of(slip_units.T, slip_scales.T)
    me = lax.axis_index("src")
    groups = lax.axis_size("src")
    portion = scenarios // groups
    side = jnp.reshape(me, (1,)).astype(jnp.int32)
    pairs = [(0, 1), (1, 0)]

    owners = lax.axis_size("rows")
    columns = green.shape[1]
    gauges_here = columns // NT
    segments = columns // SEG
    chunks = max(c for c in (1, 2, 4) if segments % c == 0)
    width = columns // chunks
    tile = SEG
    per_chunk = gauges_here // chunks
    order = arrival_order(owners)
    lag = 2 if chunks > 2 else 0
    mines, receiveds, peaks = [], [], [None] * chunks
    for c in range(chunks):
        if lag and c >= lag:
            other, mine, peaks[c - lag] = fused_of(
                side, slip_t, green, c, width, mines[c - lag], receiveds[c - lag]
            )
        else:
            other, mine = partials_of(side, slip_t, green, c, width, tile)
        mines.append(mine)
        receiveds.append(lax.ppermute(other, "src", pairs))
    for c in range(chunks):
        if peaks[c] is None:
            peaks[c] = peaks_of(mines[c], receiveds[c])
    split = (chunks + 1) // 2
    bundles = [list(range(split)), list(range(split, chunks))] if chunks > 1 else [[0]]
    pieces, ids = [], []
    for bundle in bundles:
        joined = jnp.concatenate([peaks[c] for c in bundle], 0) if len(bundle) > 1 else peaks[bundle[0]]
        pieces.append(gather_rows(joined, owners))
        local = np.concatenate([c * per_chunk + np.arange(per_chunk) for c in bundle])
        ids.append((np.asarray(order)[:, None] * gauges_here + local[None, :]).reshape(-1))
    gauge_ids = jnp.asarray(np.concatenate(ids).astype(np.int32))

    tile_total = coast_gauges.shape[0]
    slot_count = coast_gauges.shape[1]
    tiles_here = tile_total // owners
    active_slot = jnp.arange(slot_count, dtype=jnp.int32)[None, :] < coast_counts[:, None]
    weights = jnp.where(active_slot, coast_amps, jnp.zeros_like(coast_amps))
    first_tile = lax.axis_index("rows") * tiles_here
    mine_gauges = lax.dynamic_slice_in_dim(coast_gauges, first_tile, tiles_here, 0)
    mine_weights = lax.dynamic_slice_in_dim(weights, first_tile, tiles_here, 0)
    matches = mine_gauges[:, :, None] == gauge_ids[None, None, :]
    tile_table = jnp.sum(jnp.where(matches, mine_weights[:, :, None], 0.0), axis=1)
    onshore = None
    start = 0
    for piece in pieces:
        span = piece.shape[0]
        term = lax.dot_general(
            piece,
            tile_table[:, start:start + span],
            (((0,), (1,)), ((), ())),
            precision=lax.Precision.HIGHEST,
            preferred_element_type=jnp.float32,
        )
        start += span
        onshore = term if onshore is None else onshore + term
    return onshore


def solution(mesh):
    in_specs = (P(None, "src"), P(None, "src"), P("src", "rows"), P(), P(), P())
    out_specs = P("src", "rows")
    return jax.shard_map(body, mesh=mesh, in_specs=in_specs, out_specs=out_specs, check_vma=False)
```

```python
import numpy as np
import jax
import jax.numpy as jnp
from jax import lax
from jax.experimental import pallas as pl
from jax.experimental.pallas import tpu as pltpu
from jax.sharding import PartitionSpec as P

NT = 240
UBLK = 125
SEG = 1920


def matmul_kernel(side_ref, other_slip_ref, mine_slip_ref, green_ref, other_ref, mine_ref):
    block = green_ref[...]
    for slip_ref, out_ref in ((other_slip_ref, other_ref), (mine_slip_ref, mine_ref)):
        product = lax.dot_general(
            block, slip_ref[...], (((0,), (0,)), ((), ())), preferred_element_type=jnp.float32
        )
        out_ref[...] = product.astype(jnp.bfloat16)


def slip_specs(sources, half):
    return [
        pl.BlockSpec((sources, half), lambda j, side: (0, 1 - side[0])),
        pl.BlockSpec((sources, half), lambda j, side: (0, side[0])),
    ]


def partials_of(side, slip_t, green, chunk, width, tile):
    sources, scenarios = slip_t.shape
    half = scenarios // 2
    steps = width // tile
    return pl.pallas_call(
        matmul_kernel,
        grid_spec=pltpu.PrefetchScalarGridSpec(
            num_scalar_prefetch=1,
            grid=(steps,),
            in_specs=slip_specs(sources, half)
            + [pl.BlockSpec((sources, tile), lambda j, side: (0, chunk * steps + j))],
            out_specs=[pl.BlockSpec((tile, half), lambda j, side: (j, 0))] * 2,
        ),
        out_shape=[jax.ShapeDtypeStruct((width, half), jnp.bfloat16)] * 2,
        cost_estimate=pl.CostEstimate(
            flops=2 * scenarios * sources * width,
            transcendentals=0,
            bytes_accessed=2 * (sources * width + scenarios * width),
        ),
    )(side, slip_t, slip_t, green)


def peak_kernel(mine_ref, recv_ref, out_ref):
    wave = mine_ref[...].astype(jnp.float32) + recv_ref[...].astype(jnp.float32)
    gauges = SEG // NT
    out_ref[...] = jnp.max(jnp.abs(wave).reshape(gauges, NT, wave.shape[1]), axis=1)


def fused_kernel(side_ref, other_slip_ref, mine_slip_ref, green_ref, mine_prev_ref, recv_prev_ref, other_ref, mine_ref, peaks_ref):
    matmul_kernel(side_ref, other_slip_ref, mine_slip_ref, green_ref, other_ref, mine_ref)
    peak_kernel(mine_prev_ref, recv_prev_ref, peaks_ref)


def fused_of(side, slip_t, green, chunk, width, mine_prev, recv_prev):
    sources, scenarios = slip_t.shape
    half = scenarios // 2
    steps = width // SEG
    gauges = SEG // NT
    return pl.pallas_call(
        fused_kernel,
        grid_spec=pltpu.PrefetchScalarGridSpec(
            num_scalar_prefetch=1,
            grid=(steps,),
            in_specs=slip_specs(sources, half)
            + [
                pl.BlockSpec((sources, SEG), lambda j, side: (0, chunk * steps + j)),
                pl.BlockSpec((SEG, half), lambda j, side: (j, 0)),
                pl.BlockSpec((SEG, half), lambda j, side: (j, 0)),
            ],
            out_specs=[
                pl.BlockSpec((SEG, half), lambda j, side: (j, 0)),
                pl.BlockSpec((SEG, half), lambda j, side: (j, 0)),
                pl.BlockSpec((gauges, half), lambda j, side: (j, 0)),
            ],
        ),
        out_shape=[
            jax.ShapeDtypeStruct((width, half), jnp.bfloat16),
            jax.ShapeDtypeStruct((width, half), jnp.bfloat16),
            jax.ShapeDtypeStruct((steps * gauges, half), jnp.float32),
        ],
        cost_estimate=pl.CostEstimate(
            flops=2 * scenarios * sources * width,
            transcendentals=0,
            bytes_accessed=2 * (sources * width + 2 * scenarios * width),
        ),
    )(side, slip_t, slip_t, green, mine_prev, recv_prev)


def peaks_of(mine, recv):
    cols, rows = mine.shape
    blocks = cols // SEG
    gauges = SEG // NT
    return pl.pallas_call(
        peak_kernel,
        grid=(blocks,),
        in_specs=[pl.BlockSpec((SEG, rows), lambda j: (j, 0))] * 2,
        out_specs=pl.BlockSpec((gauges, rows), lambda j: (j, 0)),
        out_shape=jax.ShapeDtypeStruct((blocks * gauges, rows), jnp.float32),
        cost_estimate=pl.CostEstimate(
            flops=3 * rows * cols, transcendentals=0, bytes_accessed=4 * rows * cols
        ),
    )(mine, recv)


def slip_kernel(units_ref, scales_ref, out_ref, acc_ref):
    for b in range(scales_ref.shape[0]):
        rows = pl.ds(b * UBLK, UBLK)
        acc_ref[rows, :] = units_ref[rows, :].astype(jnp.float32) * scales_ref[b:b + 1, :]
    out_ref[...] = acc_ref[...].astype(jnp.bfloat16)


def slip_of(units_t, scales_t):
    sources, scenarios = units_t.shape
    blocks = scales_t.shape[0]
    lanes = 128 if scenarios % 128 == 0 else scenarios
    return pl.pallas_call(
        slip_kernel,
        grid=(scenarios // lanes,),
        in_specs=[
            pl.BlockSpec((sources, lanes), lambda j: (0, j)),
            pl.BlockSpec((blocks, lanes), lambda j: (0, j)),
        ],
        out_specs=pl.BlockSpec((sources, lanes), lambda j: (0, j)),
        out_shape=jax.ShapeDtypeStruct((sources, scenarios), jnp.bfloat16),
        scratch_shapes=[pltpu.VMEM((sources, lanes), jnp.float32)],
    )(units_t, scales_t)


def doubling_masks(owners):
    masks = []
    m = 1
    while m < owners:
        masks.append(m)
        m *= 2
    return masks[::-1]


def gather_rows(block, owners):
    me = lax.axis_index("rows")
    held = block.astype(jnp.bfloat16)
    for m in doubling_masks(owners):
        pairs = [(i, i ^ m) for i in range(owners)]
        got = lax.ppermute(held, "rows", pairs)
        upper = (me & m) != 0
        held = jnp.where(
            upper, jnp.concatenate([got, held], 0), jnp.concatenate([held, got], 0)
        )
    return held.astype(jnp.float32)


def arrival_order(owners):
    order = [0]
    for m in doubling_masks(owners):
        order = order + [d ^ m for d in order]
    return order


def body(slip_units, slip_scales, green, coast_gauges, coast_amps, coast_counts):
    scenarios = slip_units.shape[0]
    slip_t = slip_of(slip_units.T, slip_scales.T)
    me = lax.axis_index("src")
    groups = lax.axis_size("src")
    portion = scenarios // groups
    side = jnp.reshape(me, (1,)).astype(jnp.int32)
    pairs = [(0, 1), (1, 0)]

    owners = lax.axis_size("rows")
    columns = green.shape[1]
    gauges_here = columns // NT
    segments = columns // SEG
    chunks = max(c for c in (1, 2, 4) if segments % c == 0)
    width = columns // chunks
    tile = SEG
    per_chunk = gauges_here // chunks
    order = arrival_order(owners)
    lag = 2 if chunks > 2 else 0
    mines, receiveds, peaks = [], [], [None] * chunks
    for c in range(chunks):
        if lag and c >= lag:
            other, mine, peaks[c - lag] = fused_of(
                side, slip_t, green, c, width, mines[c - lag], receiveds[c - lag]
            )
        else:
            other, mine = partials_of(side, slip_t, green, c, width, tile)
        mines.append(mine)
        receiveds.append(lax.ppermute(other, "src", pairs))
    for c in range(chunks):
        if peaks[c] is None:
            peaks[c] = peaks_of(mines[c], receiveds[c])
    split = (chunks + 1) // 2
    bundles = [list(range(split)), list(range(split, chunks))] if chunks > 1 else [[0]]
    pieces, ids = [], []
    for bundle in bundles:
        joined = jnp.concatenate([peaks[c] for c in bundle], 0) if len(bundle) > 1 else peaks[bundle[0]]
        pieces.append(gather_rows(joined, owners))
        local = np.concatenate([c * per_chunk + np.arange(per_chunk) for c in bundle])
        ids.append((np.asarray(order)[:, None] * gauges_here + local[None, :]).reshape(-1))
    gauge_ids = jnp.asarray(np.concatenate(ids).astype(np.int32))

    tile_total = coast_gauges.shape[0]
    slot_count = coast_gauges.shape[1]
    tiles_here = tile_total // owners
    active_slot = jnp.arange(slot_count, dtype=jnp.int32)[None, :] < coast_counts[:, None]
    weights = jnp.where(active_slot, coast_amps, jnp.zeros_like(coast_amps))
    first_tile = lax.axis_index("rows") * tiles_here
    mine_gauges = lax.dynamic_slice_in_dim(coast_gauges, first_tile, tiles_here, 0)
    mine_weights = lax.dynamic_slice_in_dim(weights, first_tile, tiles_here, 0)
    matches = mine_gauges[:, :, None] == gauge_ids[None, None, :]
    tile_table = jnp.sum(jnp.where(matches, mine_weights[:, :, None], 0.0), axis=1)
    onshore = None
    start = 0
    for piece in pieces:
        span = piece.shape[0]
        term = lax.dot_general(
            piece,
            tile_table[:, start:start + span],
            (((0,), (1,)), ((), ())),
            precision=lax.Precision.HIGHEST,
            preferred_element_type=jnp.float32,
        )
        start += span
        onshore = term if onshore is None else onshore + term
    return onshore


def solution(mesh):
    in_specs = (P(None, "src"), P(None, "src"), P("src", "rows"), P(), P(), P())
    out_specs = P("src", "rows")
    return jax.shard_map(body, mesh=mesh, in_specs=in_specs, out_specs=out_specs, check_vma=False)
```

```python
import numpy as np
import jax
import jax.numpy as jnp
from jax import lax
from jax.experimental import pallas as pl
from jax.experimental.pallas import tpu as pltpu
from jax.sharding import PartitionSpec as P

NT = 240
UBLK = 125
SEG = 1920


def matmul_kernel(side_ref, other_slip_ref, mine_slip_ref, green_ref, other_ref, mine_ref):
    block = green_ref[...]
    for slip_ref, out_ref in ((other_slip_ref, other_ref), (mine_slip_ref, mine_ref)):
        product = lax.dot_general(
            block, slip_ref[...], (((0,), (0,)), ((), ())), preferred_element_type=jnp.float32
        )
        out_ref[...] = product.astype(jnp.bfloat16)


def slip_specs(sources, half):
    return [
        pl.BlockSpec((sources, half), lambda j, side: (0, 1 - side[0])),
        pl.BlockSpec((sources, half), lambda j, side: (0, side[0])),
    ]


def partials_of(side, slip_t, green, chunk, width, tile):
    sources, scenarios = slip_t.shape
    half = scenarios // 2
    steps = width // tile
    return pl.pallas_call(
        matmul_kernel,
        grid_spec=pltpu.PrefetchScalarGridSpec(
            num_scalar_prefetch=1,
            grid=(steps,),
            in_specs=slip_specs(sources, half)
            + [pl.BlockSpec((sources, tile), lambda j, side: (0, chunk * steps + j))],
            out_specs=[pl.BlockSpec((tile, half), lambda j, side: (j, 0))] * 2,
        ),
        out_shape=[jax.ShapeDtypeStruct((width, half), jnp.bfloat16)] * 2,
        cost_estimate=pl.CostEstimate(
            flops=2 * scenarios * sources * width,
            transcendentals=0,
            bytes_accessed=2 * (sources * width + scenarios * width),
        ),
    )(side, slip_t, slip_t, green)


def peak_kernel(mine_ref, recv_ref, out_ref):
    wave = mine_ref[...].astype(jnp.float32) + recv_ref[...].astype(jnp.float32)
    gauges = SEG // NT
    out_ref[...] = jnp.max(jnp.abs(wave).reshape(gauges, NT, wave.shape[1]), axis=1)


def fused_kernel(side_ref, other_slip_ref, mine_slip_ref, green_ref, mine_prev_ref, recv_prev_ref, other_ref, mine_ref, peaks_ref):
    matmul_kernel(side_ref, other_slip_ref, mine_slip_ref, green_ref, other_ref, mine_ref)
    peak_kernel(mine_prev_ref, recv_prev_ref, peaks_ref)


def fused_of(side, slip_t, green, chunk, width, mine_prev, recv_prev):
    sources, scenarios = slip_t.shape
    half = scenarios // 2
    steps = width // SEG
    gauges = SEG // NT
    return pl.pallas_call(
        fused_kernel,
        grid_spec=pltpu.PrefetchScalarGridSpec(
            num_scalar_prefetch=1,
            grid=(steps,),
            in_specs=slip_specs(sources, half)
            + [
                pl.BlockSpec((sources, SEG), lambda j, side: (0, chunk * steps + j)),
                pl.BlockSpec((SEG, half), lambda j, side: (j, 0)),
                pl.BlockSpec((SEG, half), lambda j, side: (j, 0)),
            ],
            out_specs=[
                pl.BlockSpec((SEG, half), lambda j, side: (j, 0)),
                pl.BlockSpec((SEG, half), lambda j, side: (j, 0)),
                pl.BlockSpec((gauges, half), lambda j, side: (j, 0)),
            ],
        ),
        out_shape=[
            jax.ShapeDtypeStruct((width, half), jnp.bfloat16),
            jax.ShapeDtypeStruct((width, half), jnp.bfloat16),
            jax.ShapeDtypeStruct((steps * gauges, half), jnp.float32),
        ],
        cost_estimate=pl.CostEstimate(
            flops=2 * scenarios * sources * width,
            transcendentals=0,
            bytes_accessed=2 * (sources * width + 2 * scenarios * width),
        ),
    )(side, slip_t, slip_t, green, mine_prev, recv_prev)


def peaks_of(mine, recv):
    cols, rows = mine.shape
    blocks = cols // SEG
    gauges = SEG // NT
    return pl.pallas_call(
        peak_kernel,
        grid=(blocks,),
        in_specs=[pl.BlockSpec((SEG, rows), lambda j: (j, 0))] * 2,
        out_specs=pl.BlockSpec((gauges, rows), lambda j: (j, 0)),
        out_shape=jax.ShapeDtypeStruct((blocks * gauges, rows), jnp.float32),
        cost_estimate=pl.CostEstimate(
            flops=3 * rows * cols, transcendentals=0, bytes_accessed=4 * rows * cols
        ),
    )(mine, recv)


def pair_kernel(mine_a, recv_a, mine_b, recv_b, out_a, out_b):
    peak_kernel(mine_a, recv_a, out_a)
    peak_kernel(mine_b, recv_b, out_b)


def pair_peaks_of(mine_a, recv_a, mine_b, recv_b):
    cols, rows = mine_a.shape
    blocks = cols // SEG
    gauges = SEG // NT
    return pl.pallas_call(
        pair_kernel,
        grid=(blocks,),
        in_specs=[pl.BlockSpec((SEG, rows), lambda j: (j, 0))] * 4,
        out_specs=[pl.BlockSpec((gauges, rows), lambda j: (j, 0))] * 2,
        out_shape=[jax.ShapeDtypeStruct((blocks * gauges, rows), jnp.float32)] * 2,
        cost_estimate=pl.CostEstimate(
            flops=6 * rows * cols, transcendentals=0, bytes_accessed=8 * rows * cols
        ),
    )(mine_a, recv_a, mine_b, recv_b)


def slip_kernel(units_ref, scales_ref, out_ref, acc_ref):
    for b in range(scales_ref.shape[0]):
        rows = pl.ds(b * UBLK, UBLK)
        acc_ref[rows, :] = units_ref[rows, :].astype(jnp.float32) * scales_ref[b:b + 1, :]
    out_ref[...] = acc_ref[...].astype(jnp.bfloat16)


def slip_of(units_t, scales_t):
    sources, scenarios = units_t.shape
    return pl.pallas_call(
        slip_kernel,
        out_shape=jax.ShapeDtypeStruct((sources, scenarios), jnp.bfloat16),
        scratch_shapes=[pltpu.VMEM((sources, scenarios), jnp.float32)],
    )(units_t, scales_t)


def doubling_masks(owners):
    masks = []
    m = 1
    while m < owners:
        masks.append(m)
        m *= 2
    return masks[::-1]


def gather_rows(block, owners):
    me = lax.axis_index("rows")
    held = block.astype(jnp.bfloat16)
    for m in doubling_masks(owners):
        pairs = [(i, i ^ m) for i in range(owners)]
        got = lax.ppermute(held, "rows", pairs)
        upper = (me & m) != 0
        held = jnp.where(
            upper, jnp.concatenate([got, held], 0), jnp.concatenate([held, got], 0)
        )
    return held.astype(jnp.float32)


def arrival_order(owners):
    order = [0]
    for m in doubling_masks(owners):
        order = order + [d ^ m for d in order]
    return order


def body(slip_units, slip_scales, green, coast_gauges, coast_amps, coast_counts):
    scenarios = slip_units.shape[0]
    slip_t = slip_of(slip_units.T, slip_scales.T)
    me = lax.axis_index("src")
    groups = lax.axis_size("src")
    portion = scenarios // groups
    side = jnp.reshape(me, (1,)).astype(jnp.int32)
    pairs = [(0, 1), (1, 0)]

    owners = lax.axis_size("rows")
    columns = green.shape[1]
    gauges_here = columns // NT
    segments = columns // SEG
    chunks = max(c for c in (1, 2, 4) if segments % c == 0)
    width = columns // chunks
    tile = SEG
    per_chunk = gauges_here // chunks
    order = arrival_order(owners)
    lag = 2 if chunks > 2 else 0
    mines, receiveds, peaks = [], [], [None] * chunks
    for c in range(chunks):
        if lag and c >= lag:
            other, mine, peaks[c - lag] = fused_of(
                side, slip_t, green, c, width, mines[c - lag], receiveds[c - lag]
            )
        else:
            other, mine = partials_of(side, slip_t, green, c, width, tile)
        mines.append(mine)
        receiveds.append(lax.ppermute(other, "src", pairs))
    waiting = [c for c in range(chunks) if peaks[c] is None]
    if len(waiting) == 2 and mines[waiting[0]].shape == mines[waiting[1]].shape:
        first, second = waiting
        peaks[first], peaks[second] = pair_peaks_of(
            mines[first], receiveds[first], mines[second], receiveds[second]
        )
    else:
        for c in waiting:
            peaks[c] = peaks_of(mines[c], receiveds[c])
    split = (chunks + 1) // 2
    bundles = [list(range(split)), list(range(split, chunks))] if chunks > 1 else [[0]]
    pieces, ids = [], []
    for bundle in bundles:
        joined = jnp.concatenate([peaks[c] for c in bundle], 0) if len(bundle) > 1 else peaks[bundle[0]]
        pieces.append(gather_rows(joined, owners))
        local = np.concatenate([c * per_chunk + np.arange(per_chunk) for c in bundle])
        ids.append((np.asarray(order)[:, None] * gauges_here + local[None, :]).reshape(-1))
    gauge_ids = jnp.asarray(np.concatenate(ids).astype(np.int32))

    tile_total = coast_gauges.shape[0]
    slot_count = coast_gauges.shape[1]
    tiles_here = tile_total // owners
    active_slot = jnp.arange(slot_count, dtype=jnp.int32)[None, :] < coast_counts[:, None]
    weights = jnp.where(active_slot, coast_amps, jnp.zeros_like(coast_amps))
    first_tile = lax.axis_index("rows") * tiles_here
    mine_gauges = lax.dynamic_slice_in_dim(coast_gauges, first_tile, tiles_here, 0)
    mine_weights = lax.dynamic_slice_in_dim(weights, first_tile, tiles_here, 0)
    matches = mine_gauges[:, :, None] == gauge_ids[None, None, :]
    tile_table = jnp.sum(jnp.where(matches, mine_weights[:, :, None], 0.0), axis=1)
    onshore = None
    start = 0
    for piece in pieces:
        span = piece.shape[0]
        term = lax.dot_general(
            piece,
            tile_table[:, start:start + span],
            (((0,), (1,)), ((), ())),
            precision=lax.Precision.HIGHEST,
            preferred_element_type=jnp.float32,
        )
        start += span
        onshore = term if onshore is None else onshore + term
    return onshore


def solution(mesh):
    in_specs = (P(None, "src"), P(None, "src"), P("src", "rows"), P(), P(), P())
    out_specs = P("src", "rows")
    return jax.shard_map(body, mesh=mesh, in_specs=in_specs, out_specs=out_specs, check_vma=False)
```

```python
import numpy as np
import jax
import jax.numpy as jnp
from jax import lax
from jax.experimental import pallas as pl
from jax.experimental.pallas import tpu as pltpu
from jax.sharding import PartitionSpec as P

NT = 240
UBLK = 125
SEG = 1920


def matmul_kernel(side_ref, other_slip_ref, mine_slip_ref, green_ref, other_ref, mine_ref):
    block = green_ref[...]
    for slip_ref, out_ref in ((other_slip_ref, other_ref), (mine_slip_ref, mine_ref)):
        product = lax.dot_general(
            block, slip_ref[...], (((0,), (0,)), ((), ())), preferred_element_type=jnp.float32
        )
        out_ref[...] = product.astype(jnp.bfloat16)


def slip_specs(sources, half):
    return [
        pl.BlockSpec((sources, half), lambda j, side: (0, 1 - side[0])),
        pl.BlockSpec((sources, half), lambda j, side: (0, side[0])),
    ]


def partials_of(side, slip_t, green, chunk, width, tile):
    sources, scenarios = slip_t.shape
    half = scenarios // 2
    steps = width // tile
    return pl.pallas_call(
        matmul_kernel,
        grid_spec=pltpu.PrefetchScalarGridSpec(
            num_scalar_prefetch=1,
            grid=(steps,),
            in_specs=slip_specs(sources, half)
            + [pl.BlockSpec((sources, tile), lambda j, side: (0, chunk * steps + j))],
            out_specs=[pl.BlockSpec((tile, half), lambda j, side: (j, 0))] * 2,
        ),
        out_shape=[jax.ShapeDtypeStruct((width, half), jnp.bfloat16)] * 2,
        cost_estimate=pl.CostEstimate(
            flops=2 * scenarios * sources * width,
            transcendentals=0,
            bytes_accessed=2 * (sources * width + scenarios * width),
        ),
    )(side, slip_t, slip_t, green)


def peak_kernel(mine_ref, recv_ref, out_ref):
    wave = mine_ref[...].astype(jnp.float32) + recv_ref[...].astype(jnp.float32)
    gauges = SEG // NT
    out_ref[...] = jnp.max(jnp.abs(wave).reshape(gauges, NT, wave.shape[1]), axis=1)


def fused_kernel(side_ref, other_slip_ref, mine_slip_ref, green_ref, mine_prev_ref, recv_prev_ref, other_ref, mine_ref, peaks_ref):
    matmul_kernel(side_ref, other_slip_ref, mine_slip_ref, green_ref, other_ref, mine_ref)
    peak_kernel(mine_prev_ref, recv_prev_ref, peaks_ref)


def fused_of(side, slip_t, green, chunk, width, mine_prev, recv_prev):
    sources, scenarios = slip_t.shape
    half = scenarios // 2
    steps = width // SEG
    gauges = SEG // NT
    return pl.pallas_call(
        fused_kernel,
        grid_spec=pltpu.PrefetchScalarGridSpec(
            num_scalar_prefetch=1,
            grid=(steps,),
            in_specs=slip_specs(sources, half)
            + [
                pl.BlockSpec((sources, SEG), lambda j, side: (0, chunk * steps + j)),
                pl.BlockSpec((SEG, half), lambda j, side: (j, 0)),
                pl.BlockSpec((SEG, half), lambda j, side: (j, 0)),
            ],
            out_specs=[
                pl.BlockSpec((SEG, half), lambda j, side: (j, 0)),
                pl.BlockSpec((SEG, half), lambda j, side: (j, 0)),
                pl.BlockSpec((gauges, half), lambda j, side: (j, 0)),
            ],
        ),
        out_shape=[
            jax.ShapeDtypeStruct((width, half), jnp.bfloat16),
            jax.ShapeDtypeStruct((width, half), jnp.bfloat16),
            jax.ShapeDtypeStruct((steps * gauges, half), jnp.float32),
        ],
        cost_estimate=pl.CostEstimate(
            flops=2 * scenarios * sources * width,
            transcendentals=0,
            bytes_accessed=2 * (sources * width + 2 * scenarios * width),
        ),
    )(side, slip_t, slip_t, green, mine_prev, recv_prev)


def peaks_of(mine, recv):
    cols, rows = mine.shape
    blocks = cols // SEG
    gauges = SEG // NT
    return pl.pallas_call(
        peak_kernel,
        grid=(blocks,),
        in_specs=[pl.BlockSpec((SEG, rows), lambda j: (j, 0))] * 2,
        out_specs=pl.BlockSpec((gauges, rows), lambda j: (j, 0)),
        out_shape=jax.ShapeDtypeStruct((blocks * gauges, rows), jnp.float32),
        cost_estimate=pl.CostEstimate(
            flops=3 * rows * cols, transcendentals=0, bytes_accessed=4 * rows * cols
        ),
    )(mine, recv)


def slip_kernel(units_ref, scales_ref, out_ref, acc_ref):
    for b in range(scales_ref.shape[0]):
        rows = pl.ds(b * UBLK, UBLK)
        acc_ref[rows, :] = units_ref[rows, :].astype(jnp.float32) * scales_ref[b:b + 1, :]
    out_ref[...] = acc_ref[...].astype(jnp.bfloat16)


def slip_of(units_t, scales_t):
    sources, scenarios = units_t.shape
    return pl.pallas_call(
        slip_kernel,
        out_shape=jax.ShapeDtypeStruct((sources, scenarios), jnp.bfloat16),
        scratch_shapes=[pltpu.VMEM((sources, scenarios), jnp.float32)],
    )(units_t, scales_t)


def doubling_masks(owners):
    masks = []
    m = 1
    while m < owners:
        masks.append(m)
        m *= 2
    return masks[::-1]


def gather_rows(block, owners):
    me = lax.axis_index("rows")
    held = block.astype(jnp.bfloat16)
    for m in doubling_masks(owners):
        pairs = [(i, i ^ m) for i in range(owners)]
        got = lax.ppermute(held, "rows", pairs)
        upper = (me & m) != 0
        held = jnp.where(
            upper, jnp.concatenate([got, held], 0), jnp.concatenate([held, got], 0)
        )
    return held.astype(jnp.float32)


def fan_levels(owners):
    levels, span = [], 1
    while span < owners:
        levels.append([d * span for d in range(1, 4) if d * span < owners])
        span *= 4
    return levels


def gather_fan(block, owners):
    held = block.astype(jnp.bfloat16)
    for masks in fan_levels(owners):
        got = [lax.ppermute(held, "rows", [(k, k ^ m) for k in range(owners)]) for m in masks]
        held = jnp.concatenate([held] + got, 0)
    return held.astype(jnp.float32)


def fan_offsets(owners):
    offsets = [0]
    for masks in fan_levels(owners):
        offsets = offsets + [x ^ m for m in masks for x in offsets]
    return offsets


def arrival_order(owners):
    order = [0]
    for m in doubling_masks(owners):
        order = order + [d ^ m for d in order]
    return order


def body(slip_units, slip_scales, green, coast_gauges, coast_amps, coast_counts):
    scenarios = slip_units.shape[0]
    slip_t = slip_of(slip_units.T, slip_scales.T)
    me = lax.axis_index("src")
    groups = lax.axis_size("src")
    portion = scenarios // groups
    side = jnp.reshape(me, (1,)).astype(jnp.int32)
    pairs = [(0, 1), (1, 0)]

    owners = lax.axis_size("rows")
    columns = green.shape[1]
    gauges_here = columns // NT
    segments = columns // SEG
    chunks = max(c for c in (1, 2, 4) if segments % c == 0)
    width = columns // chunks
    tile = SEG
    per_chunk = gauges_here // chunks
    order = arrival_order(owners)
    lag = 2 if chunks > 2 else 0
    mines, receiveds, peaks = [], [], [None] * chunks
    for c in range(chunks):
        if lag and c >= lag:
            other, mine, peaks[c - lag] = fused_of(
                side, slip_t, green, c, width, mines[c - lag], receiveds[c - lag]
            )
        else:
            other, mine = partials_of(side, slip_t, green, c, width, tile)
        mines.append(mine)
        receiveds.append(lax.ppermute(other, "src", pairs))
    for c in range(chunks):
        if peaks[c] is None:
            peaks[c] = peaks_of(mines[c], receiveds[c])
    split = (chunks + 1) // 2
    bundles = [list(range(split)), list(range(split, chunks))] if chunks > 1 else [[0]]
    pieces, ids = [], []
    row_me = lax.axis_index("rows")
    for b, bundle in enumerate(bundles):
        joined = jnp.concatenate([peaks[c] for c in bundle], 0) if len(bundle) > 1 else peaks[bundle[0]]
        local = np.concatenate([c * per_chunk + np.arange(per_chunk) for c in bundle])
        if b == len(bundles) - 1 and len(bundles) > 1:
            pieces.append(gather_fan(joined, owners))
            sources_at = jnp.bitwise_xor(row_me, jnp.asarray(np.asarray(fan_offsets(owners), np.int32)))
            ids.append((sources_at[:, None] * gauges_here + jnp.asarray(local.astype(np.int32))[None, :]).reshape(-1))
        else:
            pieces.append(gather_rows(joined, owners))
            ids.append(jnp.asarray((np.asarray(order)[:, None] * gauges_here + local[None, :]).reshape(-1).astype(np.int32)))
    gauge_ids = jnp.concatenate(ids)

    tile_total = coast_gauges.shape[0]
    slot_count = coast_gauges.shape[1]
    tiles_here = tile_total // owners
    active_slot = jnp.arange(slot_count, dtype=jnp.int32)[None, :] < coast_counts[:, None]
    weights = jnp.where(active_slot, coast_amps, jnp.zeros_like(coast_amps))
    first_tile = lax.axis_index("rows") * tiles_here
    mine_gauges = lax.dynamic_slice_in_dim(coast_gauges, first_tile, tiles_here, 0)
    mine_weights = lax.dynamic_slice_in_dim(weights, first_tile, tiles_here, 0)
    matches = mine_gauges[:, :, None] == gauge_ids[None, None, :]
    tile_table = jnp.sum(jnp.where(matches, mine_weights[:, :, None], 0.0), axis=1)
    onshore = None
    start = 0
    for piece in pieces:
        span = piece.shape[0]
        term = lax.dot_general(
            piece,
            tile_table[:, start:start + span],
            (((0,), (1,)), ((), ())),
            precision=lax.Precision.HIGHEST,
            preferred_element_type=jnp.float32,
        )
        start += span
        onshore = term if onshore is None else onshore + term
    return onshore


def solution(mesh):
    in_specs = (P(None, "src"), P(None, "src"), P("src", "rows"), P(), P(), P())
    out_specs = P("src", "rows")
    return jax.shard_map(body, mesh=mesh, in_specs=in_specs, out_specs=out_specs, check_vma=False)
```

```python
import numpy as np
import jax
import jax.numpy as jnp
from jax import lax
from jax.experimental import pallas as pl
from jax.experimental.pallas import tpu as pltpu
from jax.sharding import PartitionSpec as P

NT = 240
UBLK = 125
SEG = 1920


def matmul_kernel(side_ref, other_slip_ref, mine_slip_ref, green_ref, other_ref, mine_ref):
    block = green_ref[...]
    for slip_ref, out_ref in ((other_slip_ref, other_ref), (mine_slip_ref, mine_ref)):
        product = lax.dot_general(
            block, slip_ref[...], (((0,), (0,)), ((), ())), preferred_element_type=jnp.float32
        )
        out_ref[...] = product.astype(jnp.bfloat16)


def slip_specs(sources, half):
    return [
        pl.BlockSpec((sources, half), lambda j, side: (0, 1 - side[0])),
        pl.BlockSpec((sources, half), lambda j, side: (0, side[0])),
    ]


def partials_of(side, slip_t, green, chunk, width, tile):
    sources, scenarios = slip_t.shape
    half = scenarios // 2
    steps = width // tile
    return pl.pallas_call(
        matmul_kernel,
        grid_spec=pltpu.PrefetchScalarGridSpec(
            num_scalar_prefetch=1,
            grid=(steps,),
            in_specs=slip_specs(sources, half)
            + [pl.BlockSpec((sources, tile), lambda j, side: (0, chunk * steps + j))],
            out_specs=[pl.BlockSpec((tile, half), lambda j, side: (j, 0))] * 2,
        ),
        out_shape=[jax.ShapeDtypeStruct((width, half), jnp.bfloat16)] * 2,
        cost_estimate=pl.CostEstimate(
            flops=2 * scenarios * sources * width,
            transcendentals=0,
            bytes_accessed=2 * (sources * width + scenarios * width),
        ),
    )(side, slip_t, slip_t, green)


def peak_kernel(mine_ref, recv_ref, out_ref):
    wave = mine_ref[...].astype(jnp.float32) + recv_ref[...].astype(jnp.float32)
    gauges = SEG // NT
    out_ref[...] = jnp.max(jnp.abs(wave).reshape(gauges, NT, wave.shape[1]), axis=1)


def fused_kernel(side_ref, other_slip_ref, mine_slip_ref, green_ref, mine_prev_ref, recv_prev_ref, other_ref, mine_ref, peaks_ref):
    matmul_kernel(side_ref, other_slip_ref, mine_slip_ref, green_ref, other_ref, mine_ref)
    peak_kernel(mine_prev_ref, recv_prev_ref, peaks_ref)


def fused_of(side, slip_t, green, chunk, width, mine_prev, recv_prev):
    sources, scenarios = slip_t.shape
    half = scenarios // 2
    steps = width // SEG
    gauges = SEG // NT
    return pl.pallas_call(
        fused_kernel,
        grid_spec=pltpu.PrefetchScalarGridSpec(
            num_scalar_prefetch=1,
            grid=(steps,),
            in_specs=slip_specs(sources, half)
            + [
                pl.BlockSpec((sources, SEG), lambda j, side: (0, chunk * steps + j)),
                pl.BlockSpec((SEG, half), lambda j, side: (j, 0)),
                pl.BlockSpec((SEG, half), lambda j, side: (j, 0)),
            ],
            out_specs=[
                pl.BlockSpec((SEG, half), lambda j, side: (j, 0)),
                pl.BlockSpec((SEG, half), lambda j, side: (j, 0)),
                pl.BlockSpec((gauges, half), lambda j, side: (j, 0)),
            ],
        ),
        out_shape=[
            jax.ShapeDtypeStruct((width, half), jnp.bfloat16),
            jax.ShapeDtypeStruct((width, half), jnp.bfloat16),
            jax.ShapeDtypeStruct((steps * gauges, half), jnp.float32),
        ],
        cost_estimate=pl.CostEstimate(
            flops=2 * scenarios * sources * width,
            transcendentals=0,
            bytes_accessed=2 * (sources * width + 2 * scenarios * width),
        ),
    )(side, slip_t, slip_t, green, mine_prev, recv_prev)


def peaks_of(mine, recv):
    cols, rows = mine.shape
    blocks = cols // SEG
    gauges = SEG // NT
    return pl.pallas_call(
        peak_kernel,
        grid=(blocks,),
        in_specs=[pl.BlockSpec((SEG, rows), lambda j: (j, 0))] * 2,
        out_specs=pl.BlockSpec((gauges, rows), lambda j: (j, 0)),
        out_shape=jax.ShapeDtypeStruct((blocks * gauges, rows), jnp.float32),
        cost_estimate=pl.CostEstimate(
            flops=3 * rows * cols, transcendentals=0, bytes_accessed=4 * rows * cols
        ),
    )(mine, recv)


def slip_kernel(units_ref, scales_ref, out_ref, acc_ref):
    for b in range(scales_ref.shape[0]):
        rows = pl.ds(b * UBLK, UBLK)
        acc_ref[rows, :] = units_ref[rows, :].astype(jnp.float32) * scales_ref[b:b + 1, :]
    out_ref[...] = acc_ref[...].astype(jnp.bfloat16)


def slip_of(units_t, scales_t):
    sources, scenarios = units_t.shape
    return pl.pallas_call(
        slip_kernel,
        out_shape=jax.ShapeDtypeStruct((sources, scenarios), jnp.bfloat16),
        scratch_shapes=[pltpu.VMEM((sources, scenarios), jnp.float32)],
    )(units_t, scales_t)


def doubling_masks(owners):
    masks = []
    m = 1
    while m < owners:
        masks.append(m)
        m *= 2
    return masks[::-1]


def gather_rows(block, owners, masks):
    me = lax.axis_index("rows")
    held = block.astype(jnp.bfloat16)
    for m in masks:
        pairs = [(i, i ^ m) for i in range(owners)]
        got = lax.ppermute(held, "rows", pairs)
        upper = (me & m) != 0
        held = jnp.where(
            upper, jnp.concatenate([got, held], 0), jnp.concatenate([held, got], 0)
        )
    return held.astype(jnp.float32)


def arrival_order(masks):
    order = [0]
    for m in masks:
        order = order + [d ^ m for d in order]
    return order


def body(slip_units, slip_scales, green, coast_gauges, coast_amps, coast_counts):
    scenarios = slip_units.shape[0]
    slip_t = slip_of(slip_units.T, slip_scales.T)
    me = lax.axis_index("src")
    groups = lax.axis_size("src")
    portion = scenarios // groups
    side = jnp.reshape(me, (1,)).astype(jnp.int32)
    pairs = [(0, 1), (1, 0)]

    owners = lax.axis_size("rows")
    columns = green.shape[1]
    gauges_here = columns // NT
    segments = columns // SEG
    chunks = max(c for c in (1, 2, 4) if segments % c == 0)
    width = columns // chunks
    tile = SEG
    per_chunk = gauges_here // chunks
    lag = 2 if chunks > 2 else 0
    mines, receiveds, peaks = [], [], [None] * chunks
    for c in range(chunks):
        if lag and c >= lag:
            other, mine, peaks[c - lag] = fused_of(
                side, slip_t, green, c, width, mines[c - lag], receiveds[c - lag]
            )
        else:
            other, mine = partials_of(side, slip_t, green, c, width, tile)
        mines.append(mine)
        receiveds.append(lax.ppermute(other, "src", pairs))
    for c in range(chunks):
        if peaks[c] is None:
            peaks[c] = peaks_of(mines[c], receiveds[c])
    split = (chunks + 1) // 2
    bundles = [list(range(split)), list(range(split, chunks))] if chunks > 1 else [[0]]
    pieces, ids = [], []
    for b, bundle in enumerate(bundles):
        masks = doubling_masks(owners)[:: (-1 if b % 2 else 1)]
        joined = jnp.concatenate([peaks[c] for c in bundle], 0) if len(bundle) > 1 else peaks[bundle[0]]
        pieces.append(gather_rows(joined, owners, masks))
        local = np.concatenate([c * per_chunk + np.arange(per_chunk) for c in bundle])
        ids.append((np.asarray(arrival_order(masks))[:, None] * gauges_here + local[None, :]).reshape(-1))
    gauge_ids = jnp.asarray(np.concatenate(ids).astype(np.int32))

    tile_total = coast_gauges.shape[0]
    slot_count = coast_gauges.shape[1]
    tiles_here = tile_total // owners
    active_slot = jnp.arange(slot_count, dtype=jnp.int32)[None, :] < coast_counts[:, None]
    weights = jnp.where(active_slot, coast_amps, jnp.zeros_like(coast_amps))
    first_tile = lax.axis_index("rows") * tiles_here
    mine_gauges = lax.dynamic_slice_in_dim(coast_gauges, first_tile, tiles_here, 0)
    mine_weights = lax.dynamic_slice_in_dim(weights, first_tile, tiles_here, 0)
    matches = mine_gauges[:, :, None] == gauge_ids[None, None, :]
    tile_table = jnp.sum(jnp.where(matches, mine_weights[:, :, None], 0.0), axis=1)
    onshore = None
    start = 0
    for piece in pieces:
        span = piece.shape[0]
        term = lax.dot_general(
            piece,
            tile_table[:, start:start + span],
            (((0,), (1,)), ((), ())),
            precision=lax.Precision.HIGHEST,
            preferred_element_type=jnp.float32,
        )
        start += span
        onshore = term if onshore is None else onshore + term
    return onshore


def solution(mesh):
    in_specs = (P(None, "src"), P(None, "src"), P("src", "rows"), P(), P(), P())
    out_specs = P("src", "rows")
    return jax.shard_map(body, mesh=mesh, in_specs=in_specs, out_specs=out_specs, check_vma=False)
```

```python
import numpy as np
import jax
import jax.numpy as jnp
from jax import lax
from jax.experimental import pallas as pl
from jax.experimental.pallas import tpu as pltpu
from jax.sharding import PartitionSpec as P

NT = 240
UBLK = 125
SEG = 1920


def matmul_kernel(side_ref, other_slip_ref, mine_slip_ref, green_ref, other_ref, mine_ref):
    block = green_ref[...]
    for slip_ref, out_ref in ((other_slip_ref, other_ref), (mine_slip_ref, mine_ref)):
        product = lax.dot_general(
            block, slip_ref[...], (((0,), (0,)), ((), ())), preferred_element_type=jnp.float32
        )
        out_ref[...] = product.astype(jnp.bfloat16)


def slip_specs(sources, half):
    return [
        pl.BlockSpec((sources, half), lambda j, side: (0, 1 - side[0])),
        pl.BlockSpec((sources, half), lambda j, side: (0, side[0])),
    ]


def partials_of(side, slip_t, green, chunk, width, tile):
    sources, scenarios = slip_t.shape
    half = scenarios // 2
    steps = width // tile
    return pl.pallas_call(
        matmul_kernel,
        grid_spec=pltpu.PrefetchScalarGridSpec(
            num_scalar_prefetch=1,
            grid=(steps,),
            in_specs=slip_specs(sources, half)
            + [pl.BlockSpec((sources, tile), lambda j, side: (0, chunk * steps + j))],
            out_specs=[pl.BlockSpec((tile, half), lambda j, side: (j, 0))] * 2,
        ),
        out_shape=[jax.ShapeDtypeStruct((width, half), jnp.bfloat16)] * 2,
        cost_estimate=pl.CostEstimate(
            flops=2 * scenarios * sources * width,
            transcendentals=0,
            bytes_accessed=2 * (sources * width + scenarios * width),
        ),
    )(side, slip_t, slip_t, green)


def peak_kernel(mine_ref, recv_ref, out_ref):
    wave = mine_ref[...].astype(jnp.float32) + recv_ref[...].astype(jnp.float32)
    gauges = SEG // NT
    out_ref[...] = jnp.max(jnp.abs(wave).reshape(gauges, NT, wave.shape[1]), axis=1)


def fused_kernel(side_ref, other_slip_ref, mine_slip_ref, green_ref, mine_prev_ref, recv_prev_ref, other_ref, mine_ref, peaks_ref):
    matmul_kernel(side_ref, other_slip_ref, mine_slip_ref, green_ref, other_ref, mine_ref)
    peak_kernel(mine_prev_ref, recv_prev_ref, peaks_ref)


def fused_of(side, slip_t, green, chunk, width, mine_prev, recv_prev):
    sources, scenarios = slip_t.shape
    half = scenarios // 2
    steps = width // SEG
    gauges = SEG // NT
    return pl.pallas_call(
        fused_kernel,
        grid_spec=pltpu.PrefetchScalarGridSpec(
            num_scalar_prefetch=1,
            grid=(steps,),
            in_specs=slip_specs(sources, half)
            + [
                pl.BlockSpec((sources, SEG), lambda j, side: (0, chunk * steps + j)),
                pl.BlockSpec((SEG, half), lambda j, side: (j, 0)),
                pl.BlockSpec((SEG, half), lambda j, side: (j, 0)),
            ],
            out_specs=[
                pl.BlockSpec((SEG, half), lambda j, side: (j, 0)),
                pl.BlockSpec((SEG, half), lambda j, side: (j, 0)),
                pl.BlockSpec((gauges, half), lambda j, side: (j, 0)),
            ],
        ),
        out_shape=[
            jax.ShapeDtypeStruct((width, half), jnp.bfloat16),
            jax.ShapeDtypeStruct((width, half), jnp.bfloat16),
            jax.ShapeDtypeStruct((steps * gauges, half), jnp.float32),
        ],
        cost_estimate=pl.CostEstimate(
            flops=2 * scenarios * sources * width,
            transcendentals=0,
            bytes_accessed=2 * (sources * width + 2 * scenarios * width),
        ),
    )(side, slip_t, slip_t, green, mine_prev, recv_prev)


def peaks_of(mine, recv):
    cols, rows = mine.shape
    blocks = cols // SEG
    gauges = SEG // NT
    return pl.pallas_call(
        peak_kernel,
        grid=(blocks,),
        in_specs=[pl.BlockSpec((SEG, rows), lambda j: (j, 0))] * 2,
        out_specs=pl.BlockSpec((gauges, rows), lambda j: (j, 0)),
        out_shape=jax.ShapeDtypeStruct((blocks * gauges, rows), jnp.float32),
        cost_estimate=pl.CostEstimate(
            flops=3 * rows * cols, transcendentals=0, bytes_accessed=4 * rows * cols
        ),
    )(mine, recv)


def slip_kernel(units_ref, scales_ref, out_ref, acc_ref):
    for b in range(scales_ref.shape[0]):
        rows = pl.ds(b * UBLK, UBLK)
        acc_ref[rows, :] = units_ref[rows, :].astype(jnp.float32) * scales_ref[b:b + 1, :]
    out_ref[...] = acc_ref[...].astype(jnp.bfloat16)


def slip_of(units_t, scales_t):
    sources, scenarios = units_t.shape
    return pl.pallas_call(
        slip_kernel,
        out_shape=jax.ShapeDtypeStruct((sources, scenarios), jnp.bfloat16),
        scratch_shapes=[pltpu.VMEM((sources, scenarios), jnp.float32)],
    )(units_t, scales_t)


def doubling_masks(owners):
    masks = []
    m = 1
    while m < owners:
        masks.append(m)
        m *= 2
    return masks[::-1]


def gather_rows(block, owners):
    me = lax.axis_index("rows")
    held = block.astype(jnp.bfloat16)
    for m in doubling_masks(owners):
        pairs = [(i, i ^ m) for i in range(owners)]
        got = lax.ppermute(held, "rows", pairs)
        upper = (me & m) != 0
        held = jnp.where(
            upper, jnp.concatenate([got, held], 0), jnp.concatenate([held, got], 0)
        )
    return held.astype(jnp.float32)


def arrival_order(owners):
    order = [0]
    for m in doubling_masks(owners):
        order = order + [d ^ m for d in order]
    return order


def body(slip_units, slip_scales, green, coast_gauges, coast_amps, coast_counts):
    scenarios = slip_units.shape[0]
    slip_t = slip_of(slip_units.T, slip_scales.T)
    me = lax.axis_index("src")
    groups = lax.axis_size("src")
    portion = scenarios // groups
    side = jnp.reshape(me, (1,)).astype(jnp.int32)
    pairs = [(0, 1), (1, 0)]

    owners = lax.axis_size("rows")
    columns = green.shape[1]
    gauges_here = columns // NT
    segments = columns // SEG
    chunks = max(c for c in (1, 2, 4) if segments % c == 0)
    width = columns // chunks
    tile = SEG
    per_chunk = gauges_here // chunks
    order = arrival_order(owners)
    lag = 2 if chunks > 2 else 0
    mines, receiveds, peaks = [], [], [None] * chunks
    for c in range(chunks):
        if lag and c >= lag:
            other, mine, peaks[c - lag] = fused_of(
                side, slip_t, green, c, width, mines[c - lag], receiveds[c - lag]
            )
        else:
            other, mine = partials_of(side, slip_t, green, c, width, tile)
        mines.append(mine)
        receiveds.append(lax.ppermute(other, "src", pairs))
    for c in range(chunks):
        if peaks[c] is None:
            peaks[c] = peaks_of(mines[c], receiveds[c])
    split = (chunks + 1) // 2
    bundles = [list(range(split)), list(range(split, chunks))] if chunks > 1 else [[0]]
    pieces, ids = [], []
    for bundle in bundles:
        joined = jnp.concatenate([peaks[c] for c in bundle], 0) if len(bundle) > 1 else peaks[bundle[0]]
        pieces.append(gather_rows(joined, owners))
        local = np.concatenate([c * per_chunk + np.arange(per_chunk) for c in bundle])
        ids.append((np.asarray(order)[:, None] * gauges_here + local[None, :]).reshape(-1))
    gauge_ids = jnp.asarray(np.concatenate(ids).astype(np.int32))

    tile_total = coast_gauges.shape[0]
    slot_count = coast_gauges.shape[1]
    tiles_here = tile_total // owners
    active_slot = jnp.arange(slot_count, dtype=jnp.int32)[None, :] < coast_counts[:, None]
    weights = jnp.where(active_slot, coast_amps, jnp.zeros_like(coast_amps))
    first_tile = lax.axis_index("rows") * tiles_here
    mine_gauges = lax.dynamic_slice_in_dim(coast_gauges, first_tile, tiles_here, 0)
    mine_weights = lax.dynamic_slice_in_dim(weights, first_tile, tiles_here, 0)
    matches = mine_gauges[:, :, None] == gauge_ids[None, None, :]
    tile_table = jnp.sum(jnp.where(matches, mine_weights[:, :, None], 0.0), axis=1)
    onshore = None
    start = 0
    for piece in pieces:
        span = piece.shape[0]
        term = lax.dot_general(
            piece,
            tile_table[:, start:start + span],
            (((0,), (1,)), ((), ())),
            precision=lax.Precision.HIGH,
            preferred_element_type=jnp.float32,
        )
        start += span
        onshore = term if onshore is None else onshore + term
    return onshore


def solution(mesh):
    in_specs = (P(None, "src"), P(None, "src"), P("src", "rows"), P(), P(), P())
    out_specs = P("src", "rows")
    return jax.shard_map(body, mesh=mesh, in_specs=in_specs, out_specs=out_specs, check_vma=False)
```
